32 devices in a mesh: tile: 8 (over z, y), tf: 4 (over x, core).
Axes of the slice: x: 2, y: 2, z: 4, core: 2. Of those that a mesh axis runs over, the one named last changes fastest.
Arguments:
- test_field: float32 [16, 3, 16, 128, 1024], P('tf', None, None, 'tile'), may hold values from -6 to 6
- register: float32 [16, 3, 16, 128, 1024], P('tf', None, None, 'tile'), may hold values from -6 to 6
- velocity: bfloat16 [3, 16, 128, 1024], P(None, 'tf', 'tile'), may hold values from -6 to 6
- shear_shift: int32 [2], replicated, may hold values from 0 to 127
Outputs:
- new_field: float32 [16, 3, 16, 128, 1024], P('tf', None, None, 'tile')
- new_register: float32 [16, 3, 16, 128, 1024], P('tf', None, None, 'tile')
The draws below stay inside these ranges and needn't reach their ends.
Inputs may be any that keep to these rules, and one draw needn't show every extreme that they name: `shear_shift`: the two offsets are independent.
All inputs are finite; a program needn't handle non-finite values.
Results may differ from the reference program's by a relative error of at most 0.0065.
Values may be sent and summed in bfloat16 or wider, within the bound.
No kernel may reach another device: no remote copies, remote signals or barrier semaphores. Data moves between devices by JAX's collectives and lax.ppermute only.
A program may use at most 256 MiB of HBM per device.

```python
import math
import jax
import jax.numpy as jnp
from jax import lax

NX = 1024
NZ = 16
TFIELDS = 16
NY = 128


def steps_of(rng, dims, split, least, largest):
    level = 1.0
    for position, shards_of in split:
        heights = jax.random.uniform(jax.random.fold_in(jax.random.fold_in(rng, 6), position), (shards_of,), jnp.float32, least / len(split), largest / len(split))
        level = level * jnp.repeat(jnp.exp(heights), dims[position] // shards_of).reshape((-1,) + (1,) * (len(dims) - 1 - position))
    return level


def centred(stream_key, extent, deviation, bound, split=(), dtype=jnp.bfloat16):
    drawn = deviation * jax.random.normal(stream_key, extent, jnp.float32)
    if split:
        drawn = drawn * steps_of(stream_key, extent, split, -0.22, 0.18)
    return jnp.clip(drawn, -bound, bound).astype(dtype)


def setup_inputs(seed: int = 0) -> dict:
    key_of = jax.random.split(jax.random.key(seed), 5)
    test_field = centred(key_of[0], (TFIELDS, 3, NZ, NY, NX), 1.0, 6.0, ((0, 4), (3, 8)), jnp.float32)
    register = centred(key_of[1], (TFIELDS, 3, NZ, NY, NX), 1.0, 6.0, ((0, 4), (3, 8)), jnp.float32)
    velocity = centred(key_of[2], (3, NZ, NY, NX), 1.0, 6.0, ((1, 4), (2, 8)))
    shear_shift = jax.random.randint(key_of[3], (2,), 0, NY).astype(jnp.int32)
    return dict(test_field=test_field, register=register, velocity=velocity, shear_shift=shear_shift)


DIFFUSIVITY = 0.1
TIME_STEP = 0.3
RK_ALPHA = -5.0 / 9.0
RK_BETA = 15.0 / 16.0
SWEEP_SPEED = 0.75
STRETCH_RATE = 0.375


def first_derivative(shifted):
    return (45.0 * (shifted(1) - shifted(-1)) - 9.0 * (shifted(2) - shifted(-2)) + (shifted(3) - shifted(-3))) / 60.0


def second_derivative(shifted):
    return (-49.0 / 18.0) * shifted(0) + 1.5 * (shifted(1) + shifted(-1)) - 0.15 * (shifted(2) + shifted(-2)) + (shifted(3) + shifted(-3)) / 90.0


def test_pattern(field_index, planes):
    height = jnp.arange(planes).astype(jnp.float32)
    wavenumber = (field_index // 4 + 1).astype(jnp.float32)
    phase = 2.0 * math.pi * wavenumber[:, None] * height[None, :] / planes
    profile = jnp.where(((field_index // 2) % 2 == 0)[:, None], jnp.cos(phase), jnp.sin(phase))
    component = field_index % 2
    selector = (jnp.arange(3)[None, :] == component[:, None]).astype(jnp.float32)
    return (selector[:, :, None] * profile[:, None, :])[:, :, :, None, None]


def cross_emf(velocity, summed):
    vel = velocity.astype(jnp.float32)
    fld = summed.astype(jnp.float32)
    emf_x = vel[1] * fld[:, 2] - vel[2] * fld[:, 1]
    emf_y = vel[2] * fld[:, 0] - vel[0] * fld[:, 2]
    emf_z = vel[0] * fld[:, 1] - vel[1] * fld[:, 0]
    return jnp.stack([emf_x, emf_y, emf_z], 1).astype(jnp.bfloat16)


def tendency(field, view, width):
    def deriv(name, axis, channel):
        def shifted(offset):
            return view(name, axis, offset, channel)
        return first_derivative(shifted)

    def second(axis):
        def shifted(offset):
            return view("field", axis, offset, slice(None))
        return second_derivative(shifted)

    curl_x = deriv("emf", 1, 2) - deriv("emf", 2, 1)
    curl_y = deriv("emf", 2, 0) - deriv("emf", 0, 2)
    curl_z = deriv("emf", 0, 1) - deriv("emf", 1, 0)
    curl = jnp.stack([curl_x, curl_y, curl_z], 1)
    laplace = second(0) + second(1) + second(2)
    field_dy = deriv("field", 1, slice(None))
    xpos = jnp.arange(width).astype(jnp.float32)
    sweep = -SWEEP_SPEED * (2.0 * xpos / (width - 1) - 1.0)
    rate = curl + DIFFUSIVITY * laplace - sweep * field_dy
    return rate.at[:, 1].add(-STRETCH_RATE * field[:, 0])


def shear_pad(array, shear_shift):
    lower = jnp.roll(array[..., NX - 3:], -shear_shift[0], axis=-2)
    upper = jnp.roll(array[..., :3], -shear_shift[1], axis=-2)
    return jnp.concatenate([lower, array, upper], axis=-1)


def reference(test_field, register, velocity, shear_shift):
    def one_field(field_index):
        field = lax.dynamic_index_in_dim(test_field, field_index, 0, keepdims=True)
        store = lax.dynamic_index_in_dim(register, field_index, 0, keepdims=True)
        pattern = test_pattern(field_index[None], NZ)
        summed = (field + pattern).astype(jnp.bfloat16)
        emf = cross_emf(velocity, summed)
        arrays = {"field": field, "emf": emf}
        padded = {"field": shear_pad(field, shear_shift), "emf": shear_pad(emf, shear_shift)}

        def view(name, axis, offset, channel):
            if axis == 0:
                return padded[name][:, channel][..., 3 + offset:3 + offset + NX].astype(jnp.float32)
            base = arrays[name][:, channel]
            if axis == 1:
                return jnp.roll(base, -offset, axis=-2).astype(jnp.float32)
            return jnp.roll(base, -offset, axis=-3).astype(jnp.float32)

        rate = tendency(field, view, NX)
        next_register = RK_ALPHA * store + TIME_STEP * rate
        next_field = field + RK_BETA * next_register
        return next_field[0], next_register[0]

    indices = jnp.arange(TFIELDS).astype(jnp.int32)
    new_field, new_register = lax.map(one_field, indices)
    return (new_field, new_register)
```

```python
import math

import jax
import jax.numpy as jnp
from jax import lax
from jax.experimental import pallas as pl
from jax.experimental.pallas import tpu as pltpu
from jax.sharding import PartitionSpec as P

DIFFUSIVITY = 0.1
TIME_STEP = 0.3
RK_ALPHA = -5.0 / 9.0
RK_BETA = 15.0 / 16.0
SWEEP_SPEED = 0.75
STRETCH_RATE = 0.375
HALO = 3
PAD = 8


def first_derivative(shifted):
    return (
        45.0 * (shifted(1) - shifted(-1))
        - 9.0 * (shifted(2) - shifted(-2))
        + (shifted(3) - shifted(-3))
    ) / 60.0


def second_derivative(shifted):
    return (
        -49.0 / 18.0 * shifted(0)
        + 1.5 * (shifted(1) + shifted(-1))
        - 0.15 * (shifted(2) + shifted(-2))
        + (shifted(3) + shifted(-3)) / 90.0
    )


def test_pattern(field_index, planes):
    height = jnp.arange(planes).astype(jnp.float32)
    wavenumber = (field_index // 4 + 1).astype(jnp.float32)
    phase = 2.0 * math.pi * wavenumber[:, None] * height[None, :] / planes
    profile = jnp.where((field_index // 2 % 2 == 0)[:, None], jnp.cos(phase), jnp.sin(phase))
    component = field_index % 2
    selector = (jnp.arange(3)[None, :] == component[:, None]).astype(jnp.float32)
    return (selector[:, :, None] * profile[:, None, :])[:, :, :, None, None]


def cross_emf(velocity, summed):
    vel = velocity.astype(jnp.float32)
    fld = summed.astype(jnp.float32)
    emf_x = vel[1] * fld[:, 2] - vel[2] * fld[:, 1]
    emf_y = vel[2] * fld[:, 0] - vel[0] * fld[:, 2]
    emf_z = vel[0] * fld[:, 1] - vel[1] * fld[:, 0]
    return jnp.stack([emf_x, emf_y, emf_z], 1).astype(jnp.bfloat16)


def _bf(x):
    return x.astype(jnp.bfloat16).astype(jnp.float32)


def make_kernel(planes, rows, width):
    ext_w = width + 256

    def kernel(pat_ref, f_ref, fb_ref, fa_ref, r_ref, v_ref, g_ref, nf_ref, nr_ref, fs, es):
        fi = pl.program_id(0)

        def fill(z, carry):
            for c in range(3):
                fs[c, z, 0:PAD, :] = fb_ref[0, c, z]
                fs[c, z, PAD : PAD + rows, :] = f_ref[0, c, z]
                fs[c, z, PAD + rows :, :] = fa_ref[0, c, z]
            s = [_bf(fs[c, z] + pat_ref[fi, c * planes + z]) for c in range(3)]
            v = [v_ref[c, z].astype(jnp.float32) for c in range(3)]
            es[0, z] = _bf(v[1] * s[2] - v[2] * s[1])
            es[1, z] = _bf(v[2] * s[0] - v[0] * s[2])
            es[2, z] = _bf(v[0] * s[1] - v[1] * s[0])
            return carry

        lax.fori_loop(0, planes, fill, 0)

        xpos = lax.broadcasted_iota(jnp.int32, (8, width), 1).astype(jnp.float32)
        sweep = -SWEEP_SPEED * (2.0 * xpos / (width - 1) - 1.0)

        def step(z, carry):
            zi = {o: lax.rem(z + o + planes, planes) for o in range(-HALO, HALO + 1)}
            for h in range(rows // 8):
                r0 = PAD + 8 * h

                def ysh(buf, c):
                    return lambda o: buf[c, z, pl.ds(r0 + o, 8), :]

                def zsh(buf, c):
                    return lambda o: buf[c, zi[o], pl.ds(r0, 8), :]

                def xsh(buf, c, gch):
                    g = g_ref[0, gch, z, pl.ds(8 * h, 8), :]
                    ext = jnp.concatenate([g, buf[c, z, pl.ds(r0, 8), :], g], axis=-1)

                    def shifted(o):
                        if o == 0:
                            return buf[c, z, pl.ds(r0, 8), :]
                        return pltpu.roll(ext, (-o) % ext_w, 1)[:, 128 : 128 + width]

                    return shifted

                curl = [
                    first_derivative(ysh(es, 2)) - first_derivative(zsh(es, 1)),
                    first_derivative(zsh(es, 0)) - first_derivative(xsh(es, 2, 5)),
                    first_derivative(xsh(es, 1, 4)) - first_derivative(ysh(es, 0)),
                ]
                centre0 = fs[0, z, pl.ds(r0, 8), :]
                for c in range(3):
                    laplace = (
                        second_derivative(xsh(fs, c, c))
                        + second_derivative(ysh(fs, c))
                        + second_derivative(zsh(fs, c))
                    )
                    field_dy = first_derivative(ysh(fs, c))
                    rate = curl[c] + DIFFUSIVITY * laplace - sweep * field_dy
                    if c == 1:
                        rate = rate + (-STRETCH_RATE) * centre0
                    reg = r_ref[0, c, z, pl.ds(8 * h, 8), :]
                    new_reg = RK_ALPHA * reg + TIME_STEP * rate
                    centre = fs[c, z, pl.ds(r0, 8), :]
                    nr_ref[0, c, z, pl.ds(8 * h, 8), :] = new_reg
                    nf_ref[0, c, z, pl.ds(8 * h, 8), :] = centre + RK_BETA * new_reg
            return carry

        lax.fori_loop(0, planes, step, 0)

    return kernel


def stencil(pat, field, fb8, fa8, register, vel32, ghost):
    fields, _, planes, rows, width = field.shape
    blk = lambda r: pl.BlockSpec((1, 3, planes, r, width), lambda f: (f, 0, 0, 0, 0))
    out_sds = jax.ShapeDtypeStruct(field.shape, jnp.float32)
    return pl.pallas_call(
        make_kernel(planes, rows, width),
        grid=(fields,),
        in_specs=[
            pl.BlockSpec(memory_space=pltpu.SMEM),
            blk(rows),
            blk(PAD),
            blk(PAD),
            blk(rows),
            pl.BlockSpec(memory_space=pltpu.VMEM),
            pl.BlockSpec((1, 6, planes, rows, 128), lambda f: (f, 0, 0, 0, 0)),
        ],
        out_specs=[blk(rows), blk(rows)],
        out_shape=[out_sds, out_sds],
        scratch_shapes=[
            pltpu.VMEM((3, planes, rows + 2 * PAD, width), jnp.float32),
            pltpu.VMEM((3, planes, rows + 2 * PAD, width), jnp.float32),
        ],
        compiler_params=pltpu.CompilerParams(
            dimension_semantics=("arbitrary",), vmem_limit_bytes=64000 * 1024
        ),
    )(pat, field, fb8, fa8, register, vel32, ghost)


def body(test_field, register, velocity, shear_shift):
    fields, _, planes, rows, width = test_field.shape
    tiles = lax.axis_size("tile")
    tile = lax.axis_index("tile")
    total_rows = tiles * rows
    up = [(i, (i + 1) % tiles) for i in range(tiles)]
    down = [((i + 1) % tiles, i) for i in range(tiles)]

    field_index = lax.axis_index("tf") * fields + jnp.arange(fields)
    pattern = test_pattern(field_index, planes)
    pat = pattern.reshape(fields, 3 * planes)

    before = lax.ppermute(test_field[..., rows - HALO :, :], "tile", up)
    after = lax.ppermute(test_field[..., :HALO, :], "tile", down)
    fb8 = jnp.pad(before, ((0, 0),) * 3 + ((PAD - HALO, 0), (0, 0)))
    fa8 = jnp.pad(after, ((0, 0),) * 3 + ((0, PAD - HALO), (0, 0)))

    vb = lax.ppermute(velocity[:, :, rows - HALO :, :], "tile", up)
    va = lax.ppermute(velocity[:, :, :HALO, :], "tile", down)
    vext = jnp.pad(
        jnp.concatenate([vb, velocity, va], axis=2),
        ((0, 0), (0, 0), (PAD - HALO, PAD - HALO), (0, 0)),
    )
    vel32 = lax.all_gather(vext, "tf", axis=1, tiled=True)

    strip_f = jnp.concatenate([test_field[..., width - HALO :], test_field[..., :HALO]], axis=-1)
    own_v = vel32[:, :, PAD : PAD + rows, :]
    strip_v = jnp.concatenate([own_v[..., width - HALO :], own_v[..., :HALO]], axis=-1)
    strip_e = cross_emf(strip_v, (strip_f + pattern).astype(jnp.bfloat16)).astype(jnp.float32)
    comb = jnp.concatenate([strip_f, strip_e], axis=1)
    packed = jnp.transpose(comb, (4, 0, 1, 2, 3)).reshape(1, 6 * fields * 6, planes * rows)
    gathered = lax.all_gather(packed, "tile", axis=0, tiled=True)
    gathered = gathered.reshape(tiles, 6, fields, 6, planes, rows)
    gathered = jnp.transpose(gathered, (1, 2, 3, 4, 0, 5)).reshape(
        6, fields, 6, planes, total_rows
    )
    doubled = jnp.concatenate([gathered, gathered], axis=-1)
    lo_start = (tile * rows + shear_shift[0]) % total_rows
    hi_start = (tile * rows + shear_shift[1]) % total_rows
    lo = lax.dynamic_slice_in_dim(doubled[:HALO], lo_start, rows, axis=4)
    hi = lax.dynamic_slice_in_dim(doubled[HALO:], hi_start, rows, axis=4)
    lo = jnp.transpose(lo, (1, 2, 3, 4, 0))
    hi = jnp.transpose(hi, (1, 2, 3, 4, 0))
    gap = jnp.zeros((fields, 6, planes, rows, 128 - 2 * HALO), jnp.float32)
    ghost = jnp.concatenate([hi, gap, lo], axis=-1)

    new_field, new_register = stencil(pat, test_field, fb8, fa8, register, vel32, ghost)
    return (new_field, new_register)


def solution(mesh):
    return jax.shard_map(
        body,
        mesh=mesh,
        in_specs=(
            P("tf", None, None, "tile", None),
            P("tf", None, None, "tile", None),
            P(None, "tf", "tile", None),
            P(),
        ),
        out_specs=(P("tf", None, None, "tile", None), P("tf", None, None, "tile", None)),
        check_vma=False,
    )
```

```python
import math

import jax
import jax.numpy as jnp
from jax import lax
from jax.experimental import pallas as pl
from jax.experimental.pallas import tpu as pltpu
from jax.sharding import PartitionSpec as P

DIFFUSIVITY = 0.1
TIME_STEP = 0.3
RK_ALPHA = -5.0 / 9.0
RK_BETA = 15.0 / 16.0
SWEEP_SPEED = 0.75
STRETCH_RATE = 0.375
HALO = 3
PAD = 8


def first_derivative(shifted):
    return (
        45.0 * (shifted(1) - shifted(-1))
        - 9.0 * (shifted(2) - shifted(-2))
        + (shifted(3) - shifted(-3))
    ) / 60.0


def second_derivative(shifted):
    return (
        -49.0 / 18.0 * shifted(0)
        + 1.5 * (shifted(1) + shifted(-1))
        - 0.15 * (shifted(2) + shifted(-2))
        + (shifted(3) + shifted(-3)) / 90.0
    )


def test_pattern(field_index, planes):
    height = jnp.arange(planes).astype(jnp.float32)
    wavenumber = (field_index // 4 + 1).astype(jnp.float32)
    phase = 2.0 * math.pi * wavenumber[:, None] * height[None, :] / planes
    profile = jnp.where((field_index // 2 % 2 == 0)[:, None], jnp.cos(phase), jnp.sin(phase))
    component = field_index % 2
    selector = (jnp.arange(3)[None, :] == component[:, None]).astype(jnp.float32)
    return (selector[:, :, None] * profile[:, None, :])[:, :, :, None, None]


def cross_emf(velocity, summed):
    vel = velocity.astype(jnp.float32)
    fld = summed.astype(jnp.float32)
    emf_x = vel[1] * fld[:, 2] - vel[2] * fld[:, 1]
    emf_y = vel[2] * fld[:, 0] - vel[0] * fld[:, 2]
    emf_z = vel[0] * fld[:, 1] - vel[1] * fld[:, 0]
    return jnp.stack([emf_x, emf_y, emf_z], 1).astype(jnp.bfloat16)


def _bf(x):
    return x.astype(jnp.bfloat16).astype(jnp.float32)


def make_kernel(planes, rows, width):
    ext_w = width + 256

    def kernel(pat_ref, f_ref, fb_ref, fa_ref, r_ref, v_ref, g_ref, nf_ref, nr_ref, fs, es):
        fi = pl.program_id(0)

        def fill(z, carry):
            for c in range(3):
                fs[c, z, 0:PAD, :] = fb_ref[0, c, z]
                fs[c, z, PAD : PAD + rows, :] = f_ref[0, c, z]
                fs[c, z, PAD + rows :, :] = fa_ref[0, c, z]
            s = [_bf(fs[c, z] + pat_ref[fi, c * planes + z]) for c in range(3)]
            v = [v_ref[c, z].astype(jnp.float32) for c in range(3)]
            es[0, z] = _bf(v[1] * s[2] - v[2] * s[1])
            es[1, z] = _bf(v[2] * s[0] - v[0] * s[2])
            es[2, z] = _bf(v[0] * s[1] - v[1] * s[0])
            return carry

        lax.fori_loop(0, planes, fill, 0)

        xpos = lax.broadcasted_iota(jnp.int32, (8, width), 1).astype(jnp.float32)
        sweep = -SWEEP_SPEED * (2.0 * xpos / (width - 1) - 1.0)

        def step(z, carry):
            zi = {o: lax.rem(z + o + planes, planes) for o in range(-HALO, HALO + 1)}
            for h in range(rows // 8):
                r0 = PAD + 8 * h

                def ysh(buf, c):
                    return lambda o: buf[c, z, pl.ds(r0 + o, 8), :]

                def zsh(buf, c):
                    return lambda o: buf[c, zi[o], pl.ds(r0, 8), :]

                def xsh(buf, c, gch):
                    g = g_ref[0, gch, z, pl.ds(8 * h, 8), :]
                    ext = jnp.concatenate([g, buf[c, z, pl.ds(r0, 8), :], g], axis=-1)

                    def shifted(o):
                        if o == 0:
                            return buf[c, z, pl.ds(r0, 8), :]
                        return pltpu.roll(ext, (-o) % ext_w, 1)[:, 128 : 128 + width]

                    return shifted

                curl = [
                    first_derivative(ysh(es, 2)) - first_derivative(zsh(es, 1)),
                    first_derivative(zsh(es, 0)) - first_derivative(xsh(es, 2, 5)),
                    first_derivative(xsh(es, 1, 4)) - first_derivative(ysh(es, 0)),
                ]
                centre0 = fs[0, z, pl.ds(r0, 8), :]
                for c in range(3):
                    laplace = (
                        second_derivative(xsh(fs, c, c))
                        + second_derivative(ysh(fs, c))
                        + second_derivative(zsh(fs, c))
                    )
                    field_dy = first_derivative(ysh(fs, c))
                    rate = curl[c] + DIFFUSIVITY * laplace - sweep * field_dy
                    if c == 1:
                        rate = rate + (-STRETCH_RATE) * centre0
                    reg = r_ref[0, c, z, pl.ds(8 * h, 8), :]
                    new_reg = RK_ALPHA * reg + TIME_STEP * rate
                    centre = fs[c, z, pl.ds(r0, 8), :]
                    nr_ref[0, c, z, pl.ds(8 * h, 8), :] = new_reg
                    nf_ref[0, c, z, pl.ds(8 * h, 8), :] = centre + RK_BETA * new_reg
            return carry

        lax.fori_loop(0, planes, step, 0)

    return kernel


def stencil(pat, field, fb8, fa8, register, vel32, ghost):
    fields, _, planes, rows, width = field.shape
    blk = lambda r: pl.BlockSpec((1, 3, planes, r, width), lambda f: (f, 0, 0, 0, 0))
    out_sds = jax.ShapeDtypeStruct(field.shape, jnp.float32)
    return pl.pallas_call(
        make_kernel(planes, rows, width),
        grid=(fields,),
        in_specs=[
            pl.BlockSpec(memory_space=pltpu.SMEM),
            blk(rows),
            blk(PAD),
            blk(PAD),
            blk(rows),
            pl.BlockSpec(memory_space=pltpu.VMEM),
            pl.BlockSpec((1, 6, planes, rows, 128), lambda f: (f, 0, 0, 0, 0)),
        ],
        out_specs=[blk(rows), blk(rows)],
        out_shape=[out_sds, out_sds],
        scratch_shapes=[
            pltpu.VMEM((3, planes, rows + 2 * PAD, width), jnp.float32),
            pltpu.VMEM((3, planes, rows + 2 * PAD, width), jnp.float32),
        ],
        compiler_params=pltpu.CompilerParams(
            dimension_semantics=("arbitrary",), vmem_limit_bytes=64000 * 1024
        ),
    )(pat, field, fb8, fa8, register, vel32, ghost)


def body(test_field, register, velocity, shear_shift):
    fields, _, planes, rows, width = test_field.shape
    tiles = lax.axis_size("tile")
    tile = lax.axis_index("tile")
    total_rows = tiles * rows
    up = [(i, (i + 1) % tiles) for i in range(tiles)]
    down = [((i + 1) % tiles, i) for i in range(tiles)]

    field_index = lax.axis_index("tf") * fields + jnp.arange(fields)
    pattern = test_pattern(field_index, planes)
    pat = pattern.reshape(fields, 3 * planes)

    halo_dt = jnp.bfloat16
    before = lax.ppermute(test_field[..., rows - HALO :, :].astype(halo_dt), "tile", up)
    after = lax.ppermute(test_field[..., :HALO, :].astype(halo_dt), "tile", down)
    fb8 = jnp.pad(before.astype(jnp.float32), ((0, 0),) * 3 + ((PAD - HALO, 0), (0, 0)))
    fa8 = jnp.pad(after.astype(jnp.float32), ((0, 0),) * 3 + ((0, PAD - HALO), (0, 0)))

    vb = lax.ppermute(velocity[:, :, rows - HALO :, :], "tile", up)
    va = lax.ppermute(velocity[:, :, :HALO, :], "tile", down)
    vext = jnp.pad(
        jnp.concatenate([vb, velocity, va], axis=2),
        ((0, 0), (0, 0), (PAD - HALO, PAD - HALO), (0, 0)),
    )
    vel32 = lax.all_gather(vext, "tf", axis=1, tiled=True)

    strip_f = jnp.concatenate([test_field[..., width - HALO :], test_field[..., :HALO]], axis=-1)
    own_v = vel32[:, :, PAD : PAD + rows, :]
    strip_v = jnp.concatenate([own_v[..., width - HALO :], own_v[..., :HALO]], axis=-1)
    strip_e = cross_emf(strip_v, (strip_f + pattern).astype(jnp.bfloat16)).astype(jnp.float32)
    comb = jnp.concatenate([strip_f, strip_e], axis=1)
    chans = HALO * fields * 6
    packed = jnp.transpose(comb, (4, 0, 1, 2, 3)).reshape(1, 2 * chans, planes * rows)
    gathered = lax.all_gather(packed, "tile", axis=0, tiled=True)
    row_of = lax.broadcasted_iota(jnp.int32, (chans, planes * rows), 1) % rows

    def select(part, shift):
        start = (tile * rows + shift) % total_rows
        first = start // rows
        offset = start % rows
        near = lax.dynamic_index_in_dim(part, first, 0, keepdims=False)
        far = lax.dynamic_index_in_dim(part, (first + 1) % tiles, 0, keepdims=False)
        near = jnp.roll(near, -offset, axis=1)
        far = jnp.roll(far, rows - offset, axis=1)
        picked = jnp.where(row_of + offset < rows, near, far)
        return picked.reshape(HALO, fields, 6, planes, rows)

    lo = select(gathered[:, :chans], shear_shift[0])
    hi = select(gathered[:, chans:], shear_shift[1])
    lane = lax.broadcasted_iota(jnp.int32, (1, 1, 1, 1, 128), 4)
    ghost = jnp.zeros((fields, 6, planes, rows, 128), jnp.float32)
    for j in range(HALO):
        ghost = jnp.where(lane == j, hi[j][..., None], ghost)
        ghost = jnp.where(lane == 128 - HALO + j, lo[j][..., None], ghost)

    new_field, new_register = stencil(pat, test_field, fb8, fa8, register, vel32, ghost)
    return (new_field, new_register)


def solution(mesh):
    return jax.shard_map(
        body,
        mesh=mesh,
        in_specs=(
            P("tf", None, None, "tile", None),
            P("tf", None, None, "tile", None),
            P(None, "tf", "tile", None),
            P(),
        ),
        out_specs=(P("tf", None, None, "tile", None), P("tf", None, None, "tile", None)),
        check_vma=False,
    )
```

```python
import math

import jax
import jax.numpy as jnp
from jax import lax
from jax.experimental import pallas as pl
from jax.experimental.pallas import tpu as pltpu
from jax.sharding import PartitionSpec as P

DIFFUSIVITY = 0.1
TIME_STEP = 0.3
RK_ALPHA = -5.0 / 9.0
RK_BETA = 15.0 / 16.0
SWEEP_SPEED = 0.75
STRETCH_RATE = 0.375
HALO = 3
PAD = 8


def first_derivative(shifted):
    return (
        45.0 * (shifted(1) - shifted(-1))
        - 9.0 * (shifted(2) - shifted(-2))
        + (shifted(3) - shifted(-3))
    ) / 60.0


def second_derivative(shifted):
    return (
        -49.0 / 18.0 * shifted(0)
        + 1.5 * (shifted(1) + shifted(-1))
        - 0.15 * (shifted(2) + shifted(-2))
        + (shifted(3) + shifted(-3)) / 90.0
    )


def test_pattern(field_index, planes):
    height = jnp.arange(planes).astype(jnp.float32)
    wavenumber = (field_index // 4 + 1).astype(jnp.float32)
    phase = 2.0 * math.pi * wavenumber[:, None] * height[None, :] / planes
    profile = jnp.where((field_index // 2 % 2 == 0)[:, None], jnp.cos(phase), jnp.sin(phase))
    component = field_index % 2
    selector = (jnp.arange(3)[None, :] == component[:, None]).astype(jnp.float32)
    return (selector[:, :, None] * profile[:, None, :])[:, :, :, None, None]


def cross_emf(velocity, summed):
    vel = velocity.astype(jnp.float32)
    fld = summed.astype(jnp.float32)
    emf_x = vel[1] * fld[:, 2] - vel[2] * fld[:, 1]
    emf_y = vel[2] * fld[:, 0] - vel[0] * fld[:, 2]
    emf_z = vel[0] * fld[:, 1] - vel[1] * fld[:, 0]
    return jnp.stack([emf_x, emf_y, emf_z], 1).astype(jnp.bfloat16)


def _bf(x):
    return x.astype(jnp.bfloat16).astype(jnp.float32)


def make_kernel(planes, rows, width):
    ext_w = width + 256

    def kernel(pat_ref, f_ref, fb_ref, fa_ref, r_ref, v_ref, g_ref, nf_ref, nr_ref, fs, es):
        fi = pl.program_id(0)

        def fill(z, carry):
            for c in range(3):
                fs[c, z, 0:PAD, :] = fb_ref[0, c, z]
                fs[c, z, PAD : PAD + rows, :] = f_ref[0, c, z]
                fs[c, z, PAD + rows :, :] = fa_ref[0, c, z]
            s = [_bf(fs[c, z] + pat_ref[fi, c * planes + z]) for c in range(3)]
            v = [v_ref[c, z].astype(jnp.float32) for c in range(3)]
            es[0, z] = _bf(v[1] * s[2] - v[2] * s[1])
            es[1, z] = _bf(v[2] * s[0] - v[0] * s[2])
            es[2, z] = _bf(v[0] * s[1] - v[1] * s[0])
            return carry

        lax.fori_loop(0, planes, fill, 0)

        xpos = lax.broadcasted_iota(jnp.int32, (8, width), 1).astype(jnp.float32)
        sweep = -SWEEP_SPEED * (2.0 * xpos / (width - 1) - 1.0)

        def step(z, carry):
            zi = {o: lax.rem(z + o + planes, planes) for o in range(-HALO, HALO + 1)}
            for h in range(rows // 8):
                r0 = PAD + 8 * h

                def ysh(buf, c):
                    return lambda o: buf[c, z, pl.ds(r0 + o, 8), :]

                def zsh(buf, c):
                    return lambda o: buf[c, zi[o], pl.ds(r0, 8), :]

                def xsh(buf, c, gch):
                    g = g_ref[0, gch, z, pl.ds(8 * h, 8), :]
                    ext = jnp.concatenate([g, buf[c, z, pl.ds(r0, 8), :], g], axis=-1)

                    def shifted(o):
                        if o == 0:
                            return buf[c, z, pl.ds(r0, 8), :]
                        return pltpu.roll(ext, (-o) % ext_w, 1)[:, 128 : 128 + width]

                    return shifted

                curl = [
                    first_derivative(ysh(es, 2)) - first_derivative(zsh(es, 1)),
                    first_derivative(zsh(es, 0)) - first_derivative(xsh(es, 2, 5)),
                    first_derivative(xsh(es, 1, 4)) - first_derivative(ysh(es, 0)),
                ]
                centre0 = fs[0, z, pl.ds(r0, 8), :]
                for c in range(3):
                    laplace = (
                        second_derivative(xsh(fs, c, c))
                        + second_derivative(ysh(fs, c))
                        + second_derivative(zsh(fs, c))
                    )
                    field_dy = first_derivative(ysh(fs, c))
                    rate = curl[c] + DIFFUSIVITY * laplace - sweep * field_dy
                    if c == 1:
                        rate = rate + (-STRETCH_RATE) * centre0
                    reg = r_ref[0, c, z, pl.ds(8 * h, 8), :]
                    new_reg = RK_ALPHA * reg + TIME_STEP * rate
                    centre = fs[c, z, pl.ds(r0, 8), :]
                    nr_ref[0, c, z, pl.ds(8 * h, 8), :] = new_reg
                    nf_ref[0, c, z, pl.ds(8 * h, 8), :] = centre + RK_BETA * new_reg
            return carry

        lax.fori_loop(0, planes, step, 0)

    return kernel


def stencil(pat, field, fb8, fa8, register, vel32, ghost):
    fields, _, planes, rows, width = field.shape
    blk = lambda r: pl.BlockSpec((1, 3, planes, r, width), lambda f: (f, 0, 0, 0, 0))
    out_sds = jax.ShapeDtypeStruct(field.shape, jnp.float32)
    return pl.pallas_call(
        make_kernel(planes, rows, width),
        grid=(fields,),
        in_specs=[
            pl.BlockSpec(memory_space=pltpu.SMEM),
            blk(rows),
            blk(PAD),
            blk(PAD),
            blk(rows),
            pl.BlockSpec(memory_space=pltpu.VMEM),
            pl.BlockSpec((1, 6, planes, rows, 128), lambda f: (f, 0, 0, 0, 0)),
        ],
        out_specs=[blk(rows), blk(rows)],
        out_shape=[out_sds, out_sds],
        scratch_shapes=[
            pltpu.VMEM((3, planes, rows + 2 * PAD, width), jnp.float32),
            pltpu.VMEM((3, planes, rows + 2 * PAD, width), jnp.float32),
        ],
        compiler_params=pltpu.CompilerParams(
            dimension_semantics=("arbitrary",), vmem_limit_bytes=64000 * 1024
        ),
    )(pat, field, fb8, fa8, register, vel32, ghost)


def body(test_field, register, velocity, shear_shift):
    fields, _, planes, rows, width = test_field.shape
    tiles = lax.axis_size("tile")
    tile = lax.axis_index("tile")
    total_rows = tiles * rows
    up = [(i, (i + 1) % tiles) for i in range(tiles)]
    down = [((i + 1) % tiles, i) for i in range(tiles)]

    field_index = lax.axis_index("tf") * fields + jnp.arange(fields)
    pattern = test_pattern(field_index, planes)
    pat = pattern.reshape(fields, 3 * planes)

    halo_dt = jnp.bfloat16
    n_f = fields * 3 * planes * HALO
    n_v = 3 * velocity.shape[1] * HALO

    def halo_rows(sl):
        f_part = test_field[..., sl, :].astype(halo_dt).reshape(n_f, width)
        v_part = velocity[:, :, sl, :].reshape(n_v, width)
        return jnp.concatenate([f_part, v_part], axis=0)

    got_b = lax.ppermute(halo_rows(slice(rows - HALO, rows)), "tile", up)
    got_a = lax.ppermute(halo_rows(slice(0, HALO)), "tile", down)
    before = got_b[:n_f].reshape(fields, 3, planes, HALO, width)
    after = got_a[:n_f].reshape(fields, 3, planes, HALO, width)
    vb = got_b[n_f:].reshape(3, velocity.shape[1], HALO, width)
    va = got_a[n_f:].reshape(3, velocity.shape[1], HALO, width)
    fb8 = jnp.pad(before.astype(jnp.float32), ((0, 0),) * 3 + ((PAD - HALO, 0), (0, 0)))
    fa8 = jnp.pad(after.astype(jnp.float32), ((0, 0),) * 3 + ((0, PAD - HALO), (0, 0)))

    vext = jnp.pad(
        jnp.concatenate([vb, velocity, va], axis=2),
        ((0, 0), (0, 0), (PAD - HALO, PAD - HALO), (0, 0)),
    )
    vel32 = lax.all_gather(vext, "tf", axis=1, tiled=True)

    strip_f = jnp.concatenate([test_field[..., width - HALO :], test_field[..., :HALO]], axis=-1)
    strip_v = jnp.concatenate([velocity[..., width - HALO :], velocity[..., :HALO]], axis=-1)
    strip_v = lax.all_gather(strip_v, "tf", axis=1, tiled=True)
    strip_e = cross_emf(strip_v, (strip_f + pattern).astype(jnp.bfloat16)).astype(jnp.float32)
    comb = jnp.concatenate([strip_f, strip_e], axis=1)
    chans = HALO * fields * 6
    packed = jnp.transpose(comb, (4, 0, 1, 2, 3)).reshape(1, 2 * chans, planes * rows)
    gathered = lax.all_gather(packed, "tile", axis=0, tiled=True)
    row_of = lax.broadcasted_iota(jnp.int32, (chans, planes * rows), 1) % rows

    def select(part, shift):
        start = (tile * rows + shift) % total_rows
        first = start // rows
        offset = start % rows
        near = lax.dynamic_index_in_dim(part, first, 0, keepdims=False)
        far = lax.dynamic_index_in_dim(part, (first + 1) % tiles, 0, keepdims=False)
        near = jnp.roll(near, -offset, axis=1)
        far = jnp.roll(far, rows - offset, axis=1)
        picked = jnp.where(row_of + offset < rows, near, far)
        return picked.reshape(HALO, fields, 6, planes, rows)

    lo = select(gathered[:, :chans], shear_shift[0])
    hi = select(gathered[:, chans:], shear_shift[1])
    lane = lax.broadcasted_iota(jnp.int32, (1, 1, 1, 1, 128), 4)
    ghost = jnp.zeros((fields, 6, planes, rows, 128), jnp.float32)
    for j in range(HALO):
        ghost = jnp.where(lane == j, hi[j][..., None], ghost)
        ghost = jnp.where(lane == 128 - HALO + j, lo[j][..., None], ghost)

    new_field, new_register = stencil(pat, test_field, fb8, fa8, register, vel32, ghost)
    return (new_field, new_register)


def solution(mesh):
    return jax.shard_map(
        body,
        mesh=mesh,
        in_specs=(
            P("tf", None, None, "tile", None),
            P("tf", None, None, "tile", None),
            P(None, "tf", "tile", None),
            P(),
        ),
        out_specs=(P("tf", None, None, "tile", None), P("tf", None, None, "tile", None)),
        check_vma=False,
    )
```

```python
import math

import jax
import jax.numpy as jnp
from jax import lax
from jax.experimental import pallas as pl
from jax.experimental.pallas import tpu as pltpu
from jax.sharding import PartitionSpec as P

DIFFUSIVITY = 0.1
TIME_STEP = 0.3
RK_ALPHA = -5.0 / 9.0
RK_BETA = 15.0 / 16.0
SWEEP_SPEED = 0.75
STRETCH_RATE = 0.375
HALO = 3
PAD = 8


def first_derivative(shifted):
    return (
        45.0 * (shifted(1) - shifted(-1))
        - 9.0 * (shifted(2) - shifted(-2))
        + (shifted(3) - shifted(-3))
    ) / 60.0


def second_derivative(shifted):
    return (
        -49.0 / 18.0 * shifted(0)
        + 1.5 * (shifted(1) + shifted(-1))
        - 0.15 * (shifted(2) + shifted(-2))
        + (shifted(3) + shifted(-3)) / 90.0
    )


def test_pattern(field_index, planes):
    height = jnp.arange(planes).astype(jnp.float32)
    wavenumber = (field_index // 4 + 1).astype(jnp.float32)
    phase = 2.0 * math.pi * wavenumber[:, None] * height[None, :] / planes
    profile = jnp.where((field_index // 2 % 2 == 0)[:, None], jnp.cos(phase), jnp.sin(phase))
    component = field_index % 2
    selector = (jnp.arange(3)[None, :] == component[:, None]).astype(jnp.float32)
    return (selector[:, :, None] * profile[:, None, :])[:, :, :, None, None]


def cross_emf(velocity, summed):
    vel = velocity.astype(jnp.float32)
    fld = summed.astype(jnp.float32)
    emf_x = vel[1] * fld[:, 2] - vel[2] * fld[:, 1]
    emf_y = vel[2] * fld[:, 0] - vel[0] * fld[:, 2]
    emf_z = vel[0] * fld[:, 1] - vel[1] * fld[:, 0]
    return jnp.stack([emf_x, emf_y, emf_z], 1).astype(jnp.bfloat16)


def _bf(x):
    return x.astype(jnp.bfloat16).astype(jnp.float32)


def make_kernel(planes, rows, width, fi, aliased):
    ext_w = width + 256

    def kernel(pat_ref, f_ref, fb_ref, fa_ref, r_ref, v_ref, g_ref, *rest):
        if aliased:
            rest = rest[2:]
        nf_ref, nr_ref, fs, es = rest

        def fill(z, carry):
            for c in range(3):
                fs[c, z, 0:PAD, :] = fb_ref[0, c, z]
                fs[c, z, PAD : PAD + rows, :] = f_ref[0, c, z]
                fs[c, z, PAD + rows :, :] = fa_ref[0, c, z]
            s = [_bf(fs[c, z] + pat_ref[fi, c * planes + z]) for c in range(3)]
            v = [v_ref[c, z].astype(jnp.float32) for c in range(3)]
            es[0, z] = _bf(v[1] * s[2] - v[2] * s[1])
            es[1, z] = _bf(v[2] * s[0] - v[0] * s[2])
            es[2, z] = _bf(v[0] * s[1] - v[1] * s[0])
            return carry

        lax.fori_loop(0, planes, fill, 0)

        xpos = lax.broadcasted_iota(jnp.int32, (8, width), 1).astype(jnp.float32)
        sweep = -SWEEP_SPEED * (2.0 * xpos / (width - 1) - 1.0)

        def step(z, carry):
            zi = {o: lax.rem(z + o + planes, planes) for o in range(-HALO, HALO + 1)}
            for h in range(rows // 8):
                r0 = PAD + 8 * h

                def ysh(buf, c):
                    return lambda o: buf[c, z, pl.ds(r0 + o, 8), :]

                def zsh(buf, c):
                    return lambda o: buf[c, zi[o], pl.ds(r0, 8), :]

                def xsh(buf, c, gch):
                    g = g_ref[0, gch, z, pl.ds(8 * h, 8), :]
                    ext = jnp.concatenate([g, buf[c, z, pl.ds(r0, 8), :], g], axis=-1)

                    def shifted(o):
                        if o == 0:
                            return buf[c, z, pl.ds(r0, 8), :]
                        return pltpu.roll(ext, (-o) % ext_w, 1)[:, 128 : 128 + width]

                    return shifted

                curl = [
                    first_derivative(ysh(es, 2)) - first_derivative(zsh(es, 1)),
                    first_derivative(zsh(es, 0)) - first_derivative(xsh(es, 2, 5)),
                    first_derivative(xsh(es, 1, 4)) - first_derivative(ysh(es, 0)),
                ]
                centre0 = fs[0, z, pl.ds(r0, 8), :]
                for c in range(3):
                    laplace = (
                        second_derivative(xsh(fs, c, c))
                        + second_derivative(ysh(fs, c))
                        + second_derivative(zsh(fs, c))
                    )
                    field_dy = first_derivative(ysh(fs, c))
                    rate = curl[c] + DIFFUSIVITY * laplace - sweep * field_dy
                    if c == 1:
                        rate = rate + (-STRETCH_RATE) * centre0
                    reg = r_ref[0, c, z, pl.ds(8 * h, 8), :]
                    new_reg = RK_ALPHA * reg + TIME_STEP * rate
                    centre = fs[c, z, pl.ds(r0, 8), :]
                    nr_ref[0, c, z, pl.ds(8 * h, 8), :] = new_reg
                    nf_ref[0, c, z, pl.ds(8 * h, 8), :] = centre + RK_BETA * new_reg
            return carry

        lax.fori_loop(0, planes, step, 0)

    return kernel


def stencil(fi, pat, field, fb8, fa8, register, vel32, ghost, prev):
    fields, _, planes, rows, width = field.shape
    blk = lambda r: pl.BlockSpec((1, 3, planes, r, width), lambda i: (fi, 0, 0, 0, 0))
    one = lambda r: pl.BlockSpec((1, 3, planes, r, width), lambda i: (0, 0, 0, 0, 0))
    out_sds = jax.ShapeDtypeStruct(field.shape, jnp.float32)
    in_specs = [
        pl.BlockSpec(memory_space=pltpu.SMEM),
        blk(rows),
        one(PAD),
        one(PAD),
        blk(rows),
        pl.BlockSpec(memory_space=pltpu.VMEM),
        pl.BlockSpec((1, 6, planes, rows, 128), lambda i: (fi, 0, 0, 0, 0)),
    ]
    args = [pat, field, fb8, fa8, register, vel32, ghost]
    aliases = {}
    if prev is not None:
        in_specs += [pl.BlockSpec(memory_space=pl.ANY)] * 2
        args += list(prev)
        aliases = {7: 0, 8: 1}
    return pl.pallas_call(
        make_kernel(planes, rows, width, fi, prev is not None),
        grid=(1,),
        in_specs=in_specs,
        out_specs=[blk(rows), blk(rows)],
        out_shape=[out_sds, out_sds],
        scratch_shapes=[
            pltpu.VMEM((3, planes, rows + 2 * PAD, width), jnp.float32),
            pltpu.VMEM((3, planes, rows + 2 * PAD, width), jnp.float32),
        ],
        input_output_aliases=aliases,
        cost_estimate=pl.CostEstimate(
            flops=200 * field.size // fields,
            transcendentals=0,
            bytes_accessed=16 * field.size // fields,
        ),
        compiler_params=pltpu.CompilerParams(
            dimension_semantics=("arbitrary",), vmem_limit_bytes=64000 * 1024
        ),
    )(*args)


def body(test_field, register, velocity, shear_shift):
    fields, _, planes, rows, width = test_field.shape
    tiles = lax.axis_size("tile")
    tile = lax.axis_index("tile")
    total_rows = tiles * rows
    up = [(i, (i + 1) % tiles) for i in range(tiles)]
    down = [((i + 1) % tiles, i) for i in range(tiles)]

    field_index = lax.axis_index("tf") * fields + jnp.arange(fields)
    pattern = test_pattern(field_index, planes)
    pat = pattern.reshape(fields, 3 * planes)

    halo_dt = jnp.bfloat16
    n_f = fields * 3 * planes * HALO
    n_v = 3 * velocity.shape[1] * HALO

    def halo_rows(f, sl):
        f_part = test_field[f, :, :, sl, :].astype(halo_dt).reshape(3 * planes * HALO, width)
        if f > 0:
            return f_part
        v_part = velocity[:, :, sl, :].reshape(n_v, width)
        return jnp.concatenate([f_part, v_part], axis=0)

    n_1 = 3 * planes * HALO
    got = []
    for f in range(fields):
        got_b = lax.ppermute(halo_rows(f, slice(rows - HALO, rows)), "tile", up)
        got_a = lax.ppermute(halo_rows(f, slice(0, HALO)), "tile", down)
        if f == 0:
            vb = got_b[n_1:].reshape(3, velocity.shape[1], HALO, width)
            va = got_a[n_1:].reshape(3, velocity.shape[1], HALO, width)
        got.append((got_b[:n_1], got_a[:n_1]))

    def padded(pair):
        before = pair[0].reshape(1, 3, planes, HALO, width).astype(jnp.float32)
        after = pair[1].reshape(1, 3, planes, HALO, width).astype(jnp.float32)
        fb = jnp.pad(before, ((0, 0),) * 3 + ((PAD - HALO, 0), (0, 0)))
        fa = jnp.pad(after, ((0, 0),) * 3 + ((0, PAD - HALO), (0, 0)))
        return fb, fa

    vext = jnp.pad(
        jnp.concatenate([vb, velocity, va], axis=2),
        ((0, 0), (0, 0), (PAD - HALO, PAD - HALO), (0, 0)),
    )
    vel32 = lax.all_gather(vext, "tf", axis=1, tiled=True)

    strip_f = jnp.concatenate([test_field[..., width - HALO :], test_field[..., :HALO]], axis=-1)
    strip_v = jnp.concatenate([velocity[..., width - HALO :], velocity[..., :HALO]], axis=-1)
    strip_v = lax.all_gather(strip_v, "tf", axis=1, tiled=True)
    strip_e = cross_emf(strip_v, (strip_f + pattern).astype(jnp.bfloat16)).astype(jnp.float32)
    comb = jnp.concatenate([strip_f, strip_e], axis=1)
    chans = HALO * fields * 6
    packed = jnp.transpose(comb, (4, 0, 1, 2, 3)).reshape(1, 2 * chans, planes * rows)
    gathered = lax.all_gather(packed, "tile", axis=0, tiled=True)
    row_of = lax.broadcasted_iota(jnp.int32, (chans, planes * rows), 1) % rows

    def select(part, shift):
        start = (tile * rows + shift) % total_rows
        first = start // rows
        offset = start % rows
        near = lax.dynamic_index_in_dim(part, first, 0, keepdims=False)
        far = lax.dynamic_index_in_dim(part, (first + 1) % tiles, 0, keepdims=False)
        near = jnp.roll(near, -offset, axis=1)
        far = jnp.roll(far, rows - offset, axis=1)
        picked = jnp.where(row_of + offset < rows, near, far)
        return picked.reshape(HALO, fields, 6, planes, rows)

    lo = select(gathered[:, :chans], shear_shift[0])
    hi = select(gathered[:, chans:], shear_shift[1])
    lane = lax.broadcasted_iota(jnp.int32, (1, 1, 1, 1, 128), 4)
    ghost = jnp.zeros((fields, 6, planes, rows, 128), jnp.float32)
    for j in range(HALO):
        ghost = jnp.where(lane == j, hi[j][..., None], ghost)
        ghost = jnp.where(lane == 128 - HALO + j, lo[j][..., None], ghost)

    prev = None
    for f in range(fields):
        pair = got[f]
        if prev is not None:
            pair, prev = lax.optimization_barrier((pair, prev))
        fb, fa = padded(pair)
        prev = stencil(f, pat, test_field, fb, fa, register, vel32, ghost, prev)
    new_field, new_register = prev
    return (new_field, new_register)


def solution(mesh):
    return jax.shard_map(
        body,
        mesh=mesh,
        in_specs=(
            P("tf", None, None, "tile", None),
            P("tf", None, None, "tile", None),
            P(None, "tf", "tile", None),
            P(),
        ),
        out_specs=(P("tf", None, None, "tile", None), P("tf", None, None, "tile", None)),
        check_vma=False,
    )
```

```python
import math

import jax
import jax.numpy as jnp
from jax import lax
from jax.experimental import pallas as pl
from jax.experimental.pallas import tpu as pltpu
from jax.sharding import PartitionSpec as P

DIFFUSIVITY = 0.1
TIME_STEP = 0.3
RK_ALPHA = -5.0 / 9.0
RK_BETA = 15.0 / 16.0
SWEEP_SPEED = 0.75
STRETCH_RATE = 0.375
HALO = 3
PAD = 8


def first_derivative(shifted):
    return (
        45.0 * (shifted(1) - shifted(-1))
        - 9.0 * (shifted(2) - shifted(-2))
        + (shifted(3) - shifted(-3))
    ) / 60.0


def second_derivative(shifted):
    return (
        -49.0 / 18.0 * shifted(0)
        + 1.5 * (shifted(1) + shifted(-1))
        - 0.15 * (shifted(2) + shifted(-2))
        + (shifted(3) + shifted(-3)) / 90.0
    )


def test_pattern(field_index, planes):
    height = jnp.arange(planes).astype(jnp.float32)
    wavenumber = (field_index // 4 + 1).astype(jnp.float32)
    phase = 2.0 * math.pi * wavenumber[:, None] * height[None, :] / planes
    profile = jnp.where((field_index // 2 % 2 == 0)[:, None], jnp.cos(phase), jnp.sin(phase))
    component = field_index % 2
    selector = (jnp.arange(3)[None, :] == component[:, None]).astype(jnp.float32)
    return (selector[:, :, None] * profile[:, None, :])[:, :, :, None, None]


def cross_emf(velocity, summed):
    vel = velocity.astype(jnp.float32)
    fld = summed.astype(jnp.float32)
    emf_x = vel[1] * fld[:, 2] - vel[2] * fld[:, 1]
    emf_y = vel[2] * fld[:, 0] - vel[0] * fld[:, 2]
    emf_z = vel[0] * fld[:, 1] - vel[1] * fld[:, 0]
    return jnp.stack([emf_x, emf_y, emf_z], 1).astype(jnp.bfloat16)


def _bf(x):
    return x.astype(jnp.bfloat16).astype(jnp.float32)


def make_kernel(planes, rows, width, fi, aliased):
    ext_w = width + 256

    def kernel(pat_ref, f_ref, fb_ref, fa_ref, r_ref, v_ref, g_ref, *rest):
        if aliased:
            rest = rest[2:]
        nf_ref, nr_ref, fs, es = rest

        def fill(z, carry):
            for c in range(3):
                fs[c, z, 0:PAD, :] = fb_ref[0, c, z]
                fs[c, z, PAD : PAD + rows, :] = f_ref[0, c, z]
                fs[c, z, PAD + rows :, :] = fa_ref[0, c, z]
            s = [_bf(fs[c, z] + pat_ref[fi, c * planes + z]) for c in range(3)]
            v = [v_ref[c, z].astype(jnp.float32) for c in range(3)]
            es[0, z] = _bf(v[1] * s[2] - v[2] * s[1])
            es[1, z] = _bf(v[2] * s[0] - v[0] * s[2])
            es[2, z] = _bf(v[0] * s[1] - v[1] * s[0])
            return carry

        z = pl.program_id(0)

        @pl.when(z == 0)
        def _():
            lax.fori_loop(0, planes, fill, 0)

        xpos = lax.broadcasted_iota(jnp.int32, (8, width), 1).astype(jnp.float32)
        sweep = -SWEEP_SPEED * (2.0 * xpos / (width - 1) - 1.0)

        def step(z):
            zi = {o: lax.rem(z + o + planes, planes) for o in range(-HALO, HALO + 1)}
            for h in range(rows // 8):
                r0 = PAD + 8 * h

                def ysh(buf, c):
                    return lambda o: buf[c, z, pl.ds(r0 + o, 8), :]

                def zsh(buf, c):
                    return lambda o: buf[c, zi[o], pl.ds(r0, 8), :]

                def xsh(buf, c, gch):
                    g = g_ref[0, gch, z, pl.ds(8 * h, 8), :]
                    ext = jnp.concatenate([g, buf[c, z, pl.ds(r0, 8), :], g], axis=-1)

                    def shifted(o):
                        if o == 0:
                            return buf[c, z, pl.ds(r0, 8), :]
                        return pltpu.roll(ext, (-o) % ext_w, 1)[:, 128 : 128 + width]

                    return shifted

                curl = [
                    first_derivative(ysh(es, 2)) - first_derivative(zsh(es, 1)),
                    first_derivative(zsh(es, 0)) - first_derivative(xsh(es, 2, 5)),
                    first_derivative(xsh(es, 1, 4)) - first_derivative(ysh(es, 0)),
                ]
                centre0 = fs[0, z, pl.ds(r0, 8), :]
                for c in range(3):
                    laplace = (
                        second_derivative(xsh(fs, c, c))
                        + second_derivative(ysh(fs, c))
                        + second_derivative(zsh(fs, c))
                    )
                    field_dy = first_derivative(ysh(fs, c))
                    rate = curl[c] + DIFFUSIVITY * laplace - sweep * field_dy
                    if c == 1:
                        rate = rate + (-STRETCH_RATE) * centre0
                    reg = r_ref[0, c, 0, pl.ds(8 * h, 8), :]
                    new_reg = RK_ALPHA * reg + TIME_STEP * rate
                    centre = fs[c, z, pl.ds(r0, 8), :]
                    nr_ref[0, c, 0, pl.ds(8 * h, 8), :] = new_reg
                    nf_ref[0, c, 0, pl.ds(8 * h, 8), :] = centre + RK_BETA * new_reg

        step(z)

    return kernel


def stencil(fi, pat, field, fb8, fa8, register, vel32, ghost, prev):
    fields, _, planes, rows, width = field.shape
    blk = lambda r: pl.BlockSpec((1, 3, planes, r, width), lambda i: (fi, 0, 0, 0, 0))
    one = lambda r: pl.BlockSpec((1, 3, planes, r, width), lambda i: (0, 0, 0, 0, 0))
    per_z = pl.BlockSpec((1, 3, 1, rows, width), lambda i: (fi, 0, i, 0, 0))
    out_sds = jax.ShapeDtypeStruct(field.shape, jnp.float32)
    in_specs = [
        pl.BlockSpec(memory_space=pltpu.SMEM),
        blk(rows),
        one(PAD),
        one(PAD),
        per_z,
        pl.BlockSpec(memory_space=pltpu.VMEM),
        pl.BlockSpec((1, 6, planes, rows, 128), lambda i: (fi, 0, 0, 0, 0)),
    ]
    args = [pat, field, fb8, fa8, register, vel32, ghost]
    aliases = {}
    if prev is not None:
        in_specs += [pl.BlockSpec(memory_space=pl.ANY)] * 2
        args += list(prev)
        aliases = {7: 0, 8: 1}
    return pl.pallas_call(
        make_kernel(planes, rows, width, fi, prev is not None),
        grid=(planes,),
        in_specs=in_specs,
        out_specs=[per_z, per_z],
        out_shape=[out_sds, out_sds],
        scratch_shapes=[
            pltpu.VMEM((3, planes, rows + 2 * PAD, width), jnp.float32),
            pltpu.VMEM((3, planes, rows + 2 * PAD, width), jnp.float32),
        ],
        input_output_aliases=aliases,
        cost_estimate=pl.CostEstimate(
            flops=200 * field.size // fields,
            transcendentals=0,
            bytes_accessed=16 * field.size // fields,
        ),
        compiler_params=pltpu.CompilerParams(
            dimension_semantics=("arbitrary",), vmem_limit_bytes=64000 * 1024
        ),
    )(*args)


def body(test_field, register, velocity, shear_shift):
    fields, _, planes, rows, width = test_field.shape
    tiles = lax.axis_size("tile")
    tile = lax.axis_index("tile")
    total_rows = tiles * rows
    up = [(i, (i + 1) % tiles) for i in range(tiles)]
    down = [((i + 1) % tiles, i) for i in range(tiles)]

    field_index = lax.axis_index("tf") * fields + jnp.arange(fields)
    pattern = test_pattern(field_index, planes)
    pat = pattern.reshape(fields, 3 * planes)

    halo_dt = jnp.bfloat16
    n_f = fields * 3 * planes * HALO
    n_v = 3 * velocity.shape[1] * HALO

    def halo_rows(f, sl):
        f_part = test_field[f, :, :, sl, :].astype(halo_dt).reshape(3 * planes * HALO, width)
        if f > 0:
            return f_part
        v_part = velocity[:, :, sl, :].reshape(n_v, width)
        return jnp.concatenate([f_part, v_part], axis=0)

    n_1 = 3 * planes * HALO
    got = []
    for f in range(fields):
        got_b = lax.ppermute(halo_rows(f, slice(rows - HALO, rows)), "tile", up)
        got_a = lax.ppermute(halo_rows(f, slice(0, HALO)), "tile", down)
        if f == 0:
            vb = got_b[n_1:].reshape(3, velocity.shape[1], HALO, width)
            va = got_a[n_1:].reshape(3, velocity.shape[1], HALO, width)
        got.append((got_b[:n_1], got_a[:n_1]))

    def padded(pair):
        before = pair[0].reshape(1, 3, planes, HALO, width).astype(jnp.float32)
        after = pair[1].reshape(1, 3, planes, HALO, width).astype(jnp.float32)
        fb = jnp.pad(before, ((0, 0),) * 3 + ((PAD - HALO, 0), (0, 0)))
        fa = jnp.pad(after, ((0, 0),) * 3 + ((0, PAD - HALO), (0, 0)))
        return fb, fa

    vext = jnp.pad(
        jnp.concatenate([vb, velocity, va], axis=2),
        ((0, 0), (0, 0), (PAD - HALO, PAD - HALO), (0, 0)),
    )
    vel32 = lax.all_gather(vext, "tf", axis=1, tiled=True)

    strip_f = jnp.concatenate([test_field[..., width - HALO :], test_field[..., :HALO]], axis=-1)
    strip_v = jnp.concatenate([velocity[..., width - HALO :], velocity[..., :HALO]], axis=-1)
    strip_v = lax.all_gather(strip_v, "tf", axis=1, tiled=True)
    strip_e = cross_emf(strip_v, (strip_f + pattern).astype(jnp.bfloat16)).astype(jnp.float32)
    comb = jnp.concatenate([strip_f, strip_e], axis=1)
    chans = HALO * fields * 6
    packed = jnp.transpose(comb, (4, 0, 1, 2, 3)).reshape(1, 2 * chans, planes * rows)
    gathered = lax.all_gather(packed, "tile", axis=0, tiled=True)
    row_of = lax.broadcasted_iota(jnp.int32, (chans, planes * rows), 1) % rows

    def select(part, shift):
        start = (tile * rows + shift) % total_rows
        first = start // rows
        offset = start % rows
        near = lax.dynamic_index_in_dim(part, first, 0, keepdims=False)
        far = lax.dynamic_index_in_dim(part, (first + 1) % tiles, 0, keepdims=False)
        near = jnp.roll(near, -offset, axis=1)
        far = jnp.roll(far, rows - offset, axis=1)
        picked = jnp.where(row_of + offset < rows, near, far)
        return picked.reshape(HALO, fields, 6, planes, rows)

    lo = select(gathered[:, :chans], shear_shift[0])
    hi = select(gathered[:, chans:], shear_shift[1])
    lane = lax.broadcasted_iota(jnp.int32, (1, 1, 1, 1, 128), 4)
    ghost = jnp.zeros((fields, 6, planes, rows, 128), jnp.float32)
    for j in range(HALO):
        ghost = jnp.where(lane == j, hi[j][..., None], ghost)
        ghost = jnp.where(lane == 128 - HALO + j, lo[j][..., None], ghost)

    prev = None
    for f in range(fields):
        pair = got[f]
        if prev is not None:
            pair, prev = lax.optimization_barrier((pair, prev))
        fb, fa = padded(pair)
        prev = stencil(f, pat, test_field, fb, fa, register, vel32, ghost, prev)
    new_field, new_register = prev
    return (new_field, new_register)


def solution(mesh):
    return jax.shard_map(
        body,
        mesh=mesh,
        in_specs=(
            P("tf", None, None, "tile", None),
            P("tf", None, None, "tile", None),
            P(None, "tf", "tile", None),
            P(),
        ),
        out_specs=(P("tf", None, None, "tile", None), P("tf", None, None, "tile", None)),
        check_vma=False,
    )
```

```python
import math

import jax
import jax.numpy as jnp
from jax import lax
from jax.experimental import pallas as pl
from jax.experimental.pallas import tpu as pltpu
from jax.sharding import PartitionSpec as P

DIFFUSIVITY = 0.1
TIME_STEP = 0.3
RK_ALPHA = -5.0 / 9.0
RK_BETA = 15.0 / 16.0
SWEEP_SPEED = 0.75
STRETCH_RATE = 0.375
HALO = 3
PAD = 8


def first_derivative(shifted):
    return (
        45.0 * (shifted(1) - shifted(-1))
        - 9.0 * (shifted(2) - shifted(-2))
        + (shifted(3) - shifted(-3))
    ) / 60.0


def second_derivative(shifted):
    return (
        -49.0 / 18.0 * shifted(0)
        + 1.5 * (shifted(1) + shifted(-1))
        - 0.15 * (shifted(2) + shifted(-2))
        + (shifted(3) + shifted(-3)) / 90.0
    )


def test_pattern(field_index, planes):
    height = jnp.arange(planes).astype(jnp.float32)
    wavenumber = (field_index // 4 + 1).astype(jnp.float32)
    phase = 2.0 * math.pi * wavenumber[:, None] * height[None, :] / planes
    profile = jnp.where((field_index // 2 % 2 == 0)[:, None], jnp.cos(phase), jnp.sin(phase))
    component = field_index % 2
    selector = (jnp.arange(3)[None, :] == component[:, None]).astype(jnp.float32)
    return (selector[:, :, None] * profile[:, None, :])[:, :, :, None, None]


def cross_emf(velocity, summed):
    vel = velocity.astype(jnp.float32)
    fld = summed.astype(jnp.float32)
    emf_x = vel[1] * fld[:, 2] - vel[2] * fld[:, 1]
    emf_y = vel[2] * fld[:, 0] - vel[0] * fld[:, 2]
    emf_z = vel[0] * fld[:, 1] - vel[1] * fld[:, 0]
    return jnp.stack([emf_x, emf_y, emf_z], 1).astype(jnp.bfloat16)


def _bf(x):
    return x.astype(jnp.bfloat16).astype(jnp.float32)


def make_kernel(planes, rows, width, fi, aliased):
    ext_w = width + 256

    def kernel(pat_ref, f_ref, fb_ref, fa_ref, r_ref, v_ref, g_ref, *rest):
        if aliased:
            rest = rest[2:]
        nf_ref, nr_ref, fs, es = rest

        def fill(z, carry):
            for c in range(3):
                fs[c, z, 0:PAD, :] = fb_ref[0, c, z]
                fs[c, z, PAD : PAD + rows, :] = f_ref[0, c, z]
                fs[c, z, PAD + rows :, :] = fa_ref[0, c, z]
            s = [_bf(fs[c, z] + pat_ref[fi, c * planes + z]) for c in range(3)]
            v = [v_ref[c, z].astype(jnp.float32) for c in range(3)]
            es[0, z] = _bf(v[1] * s[2] - v[2] * s[1])
            es[1, z] = _bf(v[2] * s[0] - v[0] * s[2])
            es[2, z] = _bf(v[0] * s[1] - v[1] * s[0])
            return carry

        z = pl.program_id(0)

        @pl.when(z == 0)
        def _():
            lax.fori_loop(0, planes, fill, 0)

        xpos = lax.broadcasted_iota(jnp.int32, (8, width), 1).astype(jnp.float32)
        sweep = -SWEEP_SPEED * (2.0 * xpos / (width - 1) - 1.0)

        def step(z):
            zi = {o: lax.rem(z + o + planes, planes) for o in range(-HALO, HALO + 1)}
            for h in range(rows // 8):
                r0 = PAD + 8 * h

                def ysh(buf, c):
                    return lambda o: buf[c, z, pl.ds(r0 + o, 8), :]

                def zsh(buf, c):
                    return lambda o: buf[c, zi[o], pl.ds(r0, 8), :]

                def xsh(buf, c, gch):
                    g = g_ref[0, gch, z, pl.ds(8 * h, 8), :]
                    ext = jnp.concatenate([g, buf[c, z, pl.ds(r0, 8), :], g], axis=-1)

                    def shifted(o):
                        if o == 0:
                            return buf[c, z, pl.ds(r0, 8), :]
                        return pltpu.roll(ext, (-o) % ext_w, 1)[:, 128 : 128 + width]

                    return shifted

                curl = [
                    first_derivative(ysh(es, 2)) - first_derivative(zsh(es, 1)),
                    first_derivative(zsh(es, 0)) - first_derivative(xsh(es, 2, 5)),
                    first_derivative(xsh(es, 1, 4)) - first_derivative(ysh(es, 0)),
                ]
                centre0 = fs[0, z, pl.ds(r0, 8), :]
                for c in range(3):
                    laplace = (
                        second_derivative(xsh(fs, c, c))
                        + second_derivative(ysh(fs, c))
                        + second_derivative(zsh(fs, c))
                    )
                    field_dy = first_derivative(ysh(fs, c))
                    rate = curl[c] + DIFFUSIVITY * laplace - sweep * field_dy
                    if c == 1:
                        rate = rate + (-STRETCH_RATE) * centre0
                    reg = r_ref[0, c, 0, pl.ds(8 * h, 8), :]
                    new_reg = RK_ALPHA * reg + TIME_STEP * rate
                    centre = fs[c, z, pl.ds(r0, 8), :]
                    nr_ref[0, c, 0, pl.ds(8 * h, 8), :] = new_reg
                    nf_ref[0, c, 0, pl.ds(8 * h, 8), :] = centre + RK_BETA * new_reg

        step(z)

    return kernel


def stencil(fi, pat, field, fb8, fa8, register, vel32, ghost, prev):
    fields, _, planes, rows, width = field.shape
    blk = lambda r: pl.BlockSpec((1, 3, planes, r, width), lambda i: (fi, 0, 0, 0, 0))
    one = lambda r: pl.BlockSpec((1, 3, planes, r, width), lambda i: (0, 0, 0, 0, 0))
    per_z = pl.BlockSpec((1, 3, 1, rows, width), lambda i: (fi, 0, i, 0, 0))
    out_sds = jax.ShapeDtypeStruct(field.shape, jnp.float32)
    in_specs = [
        pl.BlockSpec(memory_space=pltpu.SMEM),
        blk(rows),
        one(PAD),
        one(PAD),
        per_z,
        pl.BlockSpec(memory_space=pltpu.VMEM),
        pl.BlockSpec((1, 6, planes, rows, 128), lambda i: (fi, 0, 0, 0, 0)),
    ]
    args = [pat, field, fb8, fa8, register, vel32, ghost]
    aliases = {}
    if prev is not None:
        in_specs += [pl.BlockSpec(memory_space=pl.ANY)] * 2
        args += list(prev)
        aliases = {7: 0, 8: 1}
    return pl.pallas_call(
        make_kernel(planes, rows, width, fi, prev is not None),
        grid=(planes,),
        in_specs=in_specs,
        out_specs=[per_z, per_z],
        out_shape=[out_sds, out_sds],
        scratch_shapes=[
            pltpu.VMEM((3, planes, rows + 2 * PAD, width), jnp.float32),
            pltpu.VMEM((3, planes, rows + 2 * PAD, width), jnp.float32),
        ],
        input_output_aliases=aliases,
        cost_estimate=pl.CostEstimate(
            flops=200 * field.size // fields,
            transcendentals=0,
            bytes_accessed=16 * field.size // fields,
        ),
        compiler_params=pltpu.CompilerParams(
            dimension_semantics=("arbitrary",), vmem_limit_bytes=64000 * 1024
        ),
    )(*args)


def body(test_field, register, velocity, shear_shift):
    fields, _, planes, rows, width = test_field.shape
    tiles = lax.axis_size("tile")
    tile = lax.axis_index("tile")
    total_rows = tiles * rows
    up = [(i, (i + 1) % tiles) for i in range(tiles)]
    down = [((i + 1) % tiles, i) for i in range(tiles)]

    field_index = lax.axis_index("tf") * fields + jnp.arange(fields)
    pattern = test_pattern(field_index, planes)
    pat = pattern.reshape(fields, 3 * planes)

    halo_dt = jnp.bfloat16
    n_f = fields * 3 * planes * HALO
    n_v = 3 * velocity.shape[1] * HALO

    def halo_rows(f, sl):
        return test_field[f, :, :, sl, :].astype(halo_dt).reshape(3 * planes * HALO, width)

    vb = lax.ppermute(velocity[:, :, rows - HALO :, :], "tile", up)
    va = lax.ppermute(velocity[:, :, :HALO, :], "tile", down)
    got = []
    for f in range(fields):
        got_b = lax.ppermute(halo_rows(f, slice(rows - HALO, rows)), "tile", up)
        got_a = lax.ppermute(halo_rows(f, slice(0, HALO)), "tile", down)
        got.append((got_b, got_a))

    def padded(pair):
        before = pair[0].reshape(1, 3, planes, HALO, width).astype(jnp.float32)
        after = pair[1].reshape(1, 3, planes, HALO, width).astype(jnp.float32)
        fb = jnp.pad(before, ((0, 0),) * 3 + ((PAD - HALO, 0), (0, 0)))
        fa = jnp.pad(after, ((0, 0),) * 3 + ((0, PAD - HALO), (0, 0)))
        return fb, fa

    vext = jnp.pad(
        jnp.concatenate([vb, velocity, va], axis=2),
        ((0, 0), (0, 0), (PAD - HALO, PAD - HALO), (0, 0)),
    )
    vel32 = lax.all_gather(vext, "tf", axis=1, tiled=True)

    strip_f = jnp.concatenate([test_field[..., width - HALO :], test_field[..., :HALO]], axis=-1)
    strip_v = jnp.concatenate([velocity[..., width - HALO :], velocity[..., :HALO]], axis=-1)
    strip_v = lax.all_gather(strip_v, "tf", axis=1, tiled=True)
    strip_e = cross_emf(strip_v, (strip_f + pattern).astype(jnp.bfloat16)).astype(jnp.float32)
    comb = jnp.concatenate([strip_f, strip_e], axis=1)
    chans = HALO * fields * 6
    packed = jnp.transpose(comb, (4, 0, 1, 2, 3)).reshape(1, 2 * chans, planes * rows)
    gathered = lax.all_gather(packed, "tile", axis=0, tiled=True)
    row_of = lax.broadcasted_iota(jnp.int32, (chans, planes * rows), 1) % rows

    def select(part, shift):
        start = (tile * rows + shift) % total_rows
        first = start // rows
        offset = start % rows
        near = lax.dynamic_index_in_dim(part, first, 0, keepdims=False)
        far = lax.dynamic_index_in_dim(part, (first + 1) % tiles, 0, keepdims=False)
        near = jnp.roll(near, -offset, axis=1)
        far = jnp.roll(far, rows - offset, axis=1)
        picked = jnp.where(row_of + offset < rows, near, far)
        return picked.reshape(HALO, fields, 6, planes, rows)

    lo = select(gathered[:, :chans], shear_shift[0])
    hi = select(gathered[:, chans:], shear_shift[1])
    lane = lax.broadcasted_iota(jnp.int32, (1, 1, 1, 1, 128), 4)
    ghost = jnp.zeros((fields, 6, planes, rows, 128), jnp.float32)
    for j in range(HALO):
        ghost = jnp.where(lane == j, hi[j][..., None], ghost)
        ghost = jnp.where(lane == 128 - HALO + j, lo[j][..., None], ghost)

    prev = None
    for f in range(fields):
        pair = got[f]
        if prev is not None:
            pair, prev = lax.optimization_barrier((pair, prev))
        fb, fa = padded(pair)
        prev = stencil(f, pat, test_field, fb, fa, register, vel32, ghost, prev)
    new_field, new_register = prev
    return (new_field, new_register)


def solution(mesh):
    return jax.shard_map(
        body,
        mesh=mesh,
        in_specs=(
            P("tf", None, None, "tile", None),
            P("tf", None, None, "tile", None),
            P(None, "tf", "tile", None),
            P(),
        ),
        out_specs=(P("tf", None, None, "tile", None), P("tf", None, None, "tile", None)),
        check_vma=False,
    )
```

```python
import math

import jax
import jax.numpy as jnp
from jax import lax
from jax.experimental import pallas as pl
from jax.experimental.pallas import tpu as pltpu
from jax.sharding import PartitionSpec as P

DIFFUSIVITY = 0.1
TIME_STEP = 0.3
RK_ALPHA = -5.0 / 9.0
RK_BETA = 15.0 / 16.0
SWEEP_SPEED = 0.75
STRETCH_RATE = 0.375
HALO = 3
PAD = 8


def first_derivative(shifted):
    return (
        45.0 * (shifted(1) - shifted(-1))
        - 9.0 * (shifted(2) - shifted(-2))
        + (shifted(3) - shifted(-3))
    ) / 60.0


def second_derivative(shifted):
    return (
        -49.0 / 18.0 * shifted(0)
        + 1.5 * (shifted(1) + shifted(-1))
        - 0.15 * (shifted(2) + shifted(-2))
        + (shifted(3) + shifted(-3)) / 90.0
    )


def test_pattern(field_index, planes):
    height = jnp.arange(planes).astype(jnp.float32)
    wavenumber = (field_index // 4 + 1).astype(jnp.float32)
    phase = 2.0 * math.pi * wavenumber[:, None] * height[None, :] / planes
    profile = jnp.where((field_index // 2 % 2 == 0)[:, None], jnp.cos(phase), jnp.sin(phase))
    component = field_index % 2
    selector = (jnp.arange(3)[None, :] == component[:, None]).astype(jnp.float32)
    return (selector[:, :, None] * profile[:, None, :])[:, :, :, None, None]


def cross_emf(velocity, summed):
    vel = velocity.astype(jnp.float32)
    fld = summed.astype(jnp.float32)
    emf_x = vel[1] * fld[:, 2] - vel[2] * fld[:, 1]
    emf_y = vel[2] * fld[:, 0] - vel[0] * fld[:, 2]
    emf_z = vel[0] * fld[:, 1] - vel[1] * fld[:, 0]
    return jnp.stack([emf_x, emf_y, emf_z], 1).astype(jnp.bfloat16)


def _bf(x):
    return x.astype(jnp.bfloat16).astype(jnp.float32)


def make_kernel(planes, rows, width, fi, aliased):
    ext_w = width + 256

    def kernel(pat_ref, f_ref, fb_ref, fa_ref, r_ref, v_ref, g_ref, *rest):
        if aliased:
            rest = rest[2:]
        nf_ref, nr_ref, fs, es = rest

        def fill(z, carry):
            for c in range(3):
                fs[c, z, 0:PAD, :] = fb_ref[0, c, z]
                fs[c, z, PAD : PAD + rows, :] = f_ref[0, c, z]
                fs[c, z, PAD + rows :, :] = fa_ref[0, c, z]
            s = [_bf(fs[c, z] + pat_ref[fi, c * planes + z]) for c in range(3)]
            v = [v_ref[c, z].astype(jnp.float32) for c in range(3)]
            es[0, z] = _bf(v[1] * s[2] - v[2] * s[1])
            es[1, z] = _bf(v[2] * s[0] - v[0] * s[2])
            es[2, z] = _bf(v[0] * s[1] - v[1] * s[0])
            return carry

        z = pl.program_id(0)

        @pl.when(z == 0)
        def _():
            lax.fori_loop(0, planes, fill, 0)

        xpos = lax.broadcasted_iota(jnp.int32, (8, width), 1).astype(jnp.float32)
        sweep = -SWEEP_SPEED * (2.0 * xpos / (width - 1) - 1.0)

        def step(z):
            zi = {o: lax.rem(z + o + planes, planes) for o in range(-HALO, HALO + 1)}
            for h in range(rows // 8):
                r0 = PAD + 8 * h

                def ysh(buf, c):
                    return lambda o: buf[c, z, pl.ds(r0 + o, 8), :]

                def zsh(buf, c):
                    return lambda o: buf[c, zi[o], pl.ds(r0, 8), :]

                def xsh(buf, c, gch):
                    g = g_ref[0, gch, z, pl.ds(8 * h, 8), :]
                    ext = jnp.concatenate([g, buf[c, z, pl.ds(r0, 8), :], g], axis=-1)

                    def shifted(o):
                        if o == 0:
                            return buf[c, z, pl.ds(r0, 8), :]
                        return pltpu.roll(ext, (-o) % ext_w, 1)[:, 128 : 128 + width]

                    return shifted

                curl = [
                    first_derivative(ysh(es, 2)) - first_derivative(zsh(es, 1)),
                    first_derivative(zsh(es, 0)) - first_derivative(xsh(es, 2, 4)),
                    first_derivative(xsh(es, 1, 3)) - first_derivative(ysh(es, 0)),
                ]
                centre0 = fs[0, z, pl.ds(r0, 8), :]
                for c in range(3):
                    laplace = (
                        second_derivative(xsh(fs, c, c))
                        + second_derivative(ysh(fs, c))
                        + second_derivative(zsh(fs, c))
                    )
                    field_dy = first_derivative(ysh(fs, c))
                    rate = curl[c] + DIFFUSIVITY * laplace - sweep * field_dy
                    if c == 1:
                        rate = rate + (-STRETCH_RATE) * centre0
                    reg = r_ref[0, c, 0, pl.ds(8 * h, 8), :]
                    new_reg = RK_ALPHA * reg + TIME_STEP * rate
                    centre = fs[c, z, pl.ds(r0, 8), :]
                    nr_ref[0, c, 0, pl.ds(8 * h, 8), :] = new_reg
                    nf_ref[0, c, 0, pl.ds(8 * h, 8), :] = centre + RK_BETA * new_reg

        step(z)

    return kernel


def stencil(fi, pat, field, fb8, fa8, register, vel32, ghost, prev):
    fields, _, planes, rows, width = field.shape
    blk = lambda r: pl.BlockSpec((1, 3, planes, r, width), lambda i: (fi, 0, 0, 0, 0))
    one = lambda r: pl.BlockSpec((1, 3, planes, r, width), lambda i: (0, 0, 0, 0, 0))
    per_z = pl.BlockSpec((1, 3, 1, rows, width), lambda i: (fi, 0, i, 0, 0))
    out_sds = jax.ShapeDtypeStruct(field.shape, jnp.float32)
    in_specs = [
        pl.BlockSpec(memory_space=pltpu.SMEM),
        blk(rows),
        one(PAD),
        one(PAD),
        per_z,
        pl.BlockSpec(memory_space=pltpu.VMEM),
        pl.BlockSpec((1, 5, planes, rows, 128), lambda i: (fi, 0, 0, 0, 0)),
    ]
    args = [pat, field, fb8, fa8, register, vel32, ghost]
    aliases = {}
    if prev is not None:
        in_specs += [pl.BlockSpec(memory_space=pl.ANY)] * 2
        args += list(prev)
        aliases = {7: 0, 8: 1}
    return pl.pallas_call(
        make_kernel(planes, rows, width, fi, prev is not None),
        grid=(planes,),
        in_specs=in_specs,
        out_specs=[per_z, per_z],
        out_shape=[out_sds, out_sds],
        scratch_shapes=[
            pltpu.VMEM((3, planes, rows + 2 * PAD, width), jnp.float32),
            pltpu.VMEM((3, planes, rows + 2 * PAD, width), jnp.float32),
        ],
        input_output_aliases=aliases,
        cost_estimate=pl.CostEstimate(
            flops=200 * field.size // fields,
            transcendentals=0,
            bytes_accessed=16 * field.size // fields,
        ),
        compiler_params=pltpu.CompilerParams(
            dimension_semantics=("arbitrary",), vmem_limit_bytes=64000 * 1024
        ),
    )(*args)


def body(test_field, register, velocity, shear_shift):
    fields, _, planes, rows, width = test_field.shape
    tiles = lax.axis_size("tile")
    tile = lax.axis_index("tile")
    total_rows = tiles * rows
    up = [(i, (i + 1) % tiles) for i in range(tiles)]
    down = [((i + 1) % tiles, i) for i in range(tiles)]

    field_index = lax.axis_index("tf") * fields + jnp.arange(fields)
    pattern = test_pattern(field_index, planes)
    pat = pattern.reshape(fields, 3 * planes)

    halo_dt = jnp.bfloat16
    n_f = fields * 3 * planes * HALO
    n_v = 3 * velocity.shape[1] * HALO

    def halo_rows(f, sl):
        return test_field[f, :, :, sl, :].astype(halo_dt).reshape(3 * planes * HALO, width)

    vb = lax.ppermute(velocity[:, :, rows - HALO :, :], "tile", up)
    va = lax.ppermute(velocity[:, :, :HALO, :], "tile", down)
    got = []
    for f in range(fields):
        got_b = lax.ppermute(halo_rows(f, slice(rows - HALO, rows)), "tile", up)
        got_a = lax.ppermute(halo_rows(f, slice(0, HALO)), "tile", down)
        got.append((got_b, got_a))

    def padded(pair):
        before = pair[0].reshape(1, 3, planes, HALO, width).astype(jnp.float32)
        after = pair[1].reshape(1, 3, planes, HALO, width).astype(jnp.float32)
        fb = jnp.pad(before, ((0, 0),) * 3 + ((PAD - HALO, 0), (0, 0)))
        fa = jnp.pad(after, ((0, 0),) * 3 + ((0, PAD - HALO), (0, 0)))
        return fb, fa

    vext = jnp.pad(
        jnp.concatenate([vb, velocity, va], axis=2),
        ((0, 0), (0, 0), (PAD - HALO, PAD - HALO), (0, 0)),
    )
    vel32 = lax.all_gather(vext, "tf", axis=1, tiled=True)

    strip_f = jnp.concatenate([test_field[..., width - HALO :], test_field[..., :HALO]], axis=-1)
    strip_v = jnp.concatenate([velocity[..., width - HALO :], velocity[..., :HALO]], axis=-1)
    strip_v = lax.all_gather(strip_v, "tf", axis=1, tiled=True)
    strip_e = cross_emf(strip_v, (strip_f + pattern).astype(jnp.bfloat16)).astype(jnp.float32)
    comb = jnp.concatenate([strip_f, strip_e[:, 1:]], axis=1).astype(jnp.bfloat16)
    chans = HALO * fields * 5
    packed = jnp.transpose(comb, (4, 0, 1, 2, 3)).reshape(1, 2 * chans, planes * rows)
    gathered = lax.all_gather(packed, "tile", axis=0, tiled=True)
    row_of = lax.broadcasted_iota(jnp.int32, (chans, planes * rows), 1) % rows

    def select(part, shift):
        start = (tile * rows + shift) % total_rows
        first = start // rows
        offset = start % rows
        near = lax.dynamic_index_in_dim(part, first, 0, keepdims=False)
        far = lax.dynamic_index_in_dim(part, (first + 1) % tiles, 0, keepdims=False)
        near = jnp.roll(near, -offset, axis=1)
        far = jnp.roll(far, rows - offset, axis=1)
        picked = jnp.where(row_of + offset < rows, near, far)
        return picked.reshape(HALO, fields, 5, planes, rows).astype(jnp.float32)

    lo = select(gathered[:, :chans], shear_shift[0])
    hi = select(gathered[:, chans:], shear_shift[1])
    lane = lax.broadcasted_iota(jnp.int32, (1, 1, 1, 1, 128), 4)
    ghost = jnp.zeros((fields, 5, planes, rows, 128), jnp.float32)
    for j in range(HALO):
        ghost = jnp.where(lane == j, hi[j][..., None], ghost)
        ghost = jnp.where(lane == 128 - HALO + j, lo[j][..., None], ghost)

    prev = None
    for f in range(fields):
        pair = got[f]
        if prev is not None:
            pair, prev = lax.optimization_barrier((pair, prev))
        fb, fa = padded(pair)
        prev = stencil(f, pat, test_field, fb, fa, register, vel32, ghost, prev)
    new_field, new_register = prev
    return (new_field, new_register)


def solution(mesh):
    return jax.shard_map(
        body,
        mesh=mesh,
        in_specs=(
            P("tf", None, None, "tile", None),
            P("tf", None, None, "tile", None),
            P(None, "tf", "tile", None),
            P(),
        ),
        out_specs=(P("tf", None, None, "tile", None), P("tf", None, None, "tile", None)),
        check_vma=False,
    )
```

```python
import math

import jax
import jax.numpy as jnp
from jax import lax
from jax.experimental import pallas as pl
from jax.experimental.pallas import tpu as pltpu
from jax.sharding import PartitionSpec as P

DIFFUSIVITY = 0.1
TIME_STEP = 0.3
RK_ALPHA = -5.0 / 9.0
RK_BETA = 15.0 / 16.0
SWEEP_SPEED = 0.75
STRETCH_RATE = 0.375
HALO = 3
PAD = 8


def first_derivative(shifted):
    return (
        45.0 * (shifted(1) - shifted(-1))
        - 9.0 * (shifted(2) - shifted(-2))
        + (shifted(3) - shifted(-3))
    ) / 60.0


def second_derivative(shifted):
    return (
        -49.0 / 18.0 * shifted(0)
        + 1.5 * (shifted(1) + shifted(-1))
        - 0.15 * (shifted(2) + shifted(-2))
        + (shifted(3) + shifted(-3)) / 90.0
    )


def test_pattern(field_index, planes):
    height = jnp.arange(planes).astype(jnp.float32)
    wavenumber = (field_index // 4 + 1).astype(jnp.float32)
    phase = 2.0 * math.pi * wavenumber[:, None] * height[None, :] / planes
    profile = jnp.where((field_index // 2 % 2 == 0)[:, None], jnp.cos(phase), jnp.sin(phase))
    component = field_index % 2
    selector = (jnp.arange(3)[None, :] == component[:, None]).astype(jnp.float32)
    return (selector[:, :, None] * profile[:, None, :])[:, :, :, None, None]


def cross_emf(velocity, summed):
    vel = velocity.astype(jnp.float32)
    fld = summed.astype(jnp.float32)
    emf_x = vel[1] * fld[:, 2] - vel[2] * fld[:, 1]
    emf_y = vel[2] * fld[:, 0] - vel[0] * fld[:, 2]
    emf_z = vel[0] * fld[:, 1] - vel[1] * fld[:, 0]
    return jnp.stack([emf_x, emf_y, emf_z], 1).astype(jnp.bfloat16)


def _bf(x):
    return x.astype(jnp.bfloat16).astype(jnp.float32)


def make_kernel(planes, rows, width, fi, aliased):
    ext_w = width + 256

    def kernel(pat_ref, f_ref, fb_ref, fa_ref, r_ref, v_ref, g_ref, *rest):
        if aliased:
            rest = rest[2:]
        nf_ref, nr_ref, fs, es = rest

        def fill_halo():
            for zz in range(planes):
                for c in range(3):
                    at = (c * planes + zz) * HALO
                    got_b = fb_ref[at : at + HALO, :].astype(jnp.float32)
                    got_a = fa_ref[at : at + HALO, :].astype(jnp.float32)
                    fs[c, zz, PAD - HALO : PAD, :] = got_b
                    fs[c, zz, PAD + rows : PAD + rows + HALO, :] = got_a

        def fill(z, carry):
            for c in range(3):
                fs[c, z, PAD : PAD + rows, :] = f_ref[0, c, z]
            s = [_bf(fs[c, z] + pat_ref[fi, c * planes + z]) for c in range(3)]
            v = [v_ref[c, z].astype(jnp.float32) for c in range(3)]
            es[0, z] = _bf(v[1] * s[2] - v[2] * s[1])
            es[1, z] = _bf(v[2] * s[0] - v[0] * s[2])
            es[2, z] = _bf(v[0] * s[1] - v[1] * s[0])
            return carry

        z = pl.program_id(0)

        @pl.when(z == 0)
        def _():
            fill_halo()
            lax.fori_loop(0, planes, fill, 0)

        xpos = lax.broadcasted_iota(jnp.int32, (8, width), 1).astype(jnp.float32)
        sweep = -SWEEP_SPEED * (2.0 * xpos / (width - 1) - 1.0)

        def step(z):
            zi = {o: lax.rem(z + o + planes, planes) for o in range(-HALO, HALO + 1)}
            for h in range(rows // 8):
                r0 = PAD + 8 * h

                def ysh(buf, c):
                    return lambda o: buf[c, z, pl.ds(r0 + o, 8), :]

                def zsh(buf, c):
                    return lambda o: buf[c, zi[o], pl.ds(r0, 8), :]

                def xsh(buf, c, gch):
                    g = g_ref[0, gch, z, pl.ds(8 * h, 8), :]
                    ext = jnp.concatenate([g, buf[c, z, pl.ds(r0, 8), :], g], axis=-1)

                    def shifted(o):
                        if o == 0:
                            return buf[c, z, pl.ds(r0, 8), :]
                        return pltpu.roll(ext, (-o) % ext_w, 1)[:, 128 : 128 + width]

                    return shifted

                curl = [
                    first_derivative(ysh(es, 2)) - first_derivative(zsh(es, 1)),
                    first_derivative(zsh(es, 0)) - first_derivative(xsh(es, 2, 5)),
                    first_derivative(xsh(es, 1, 4)) - first_derivative(ysh(es, 0)),
                ]
                centre0 = fs[0, z, pl.ds(r0, 8), :]
                for c in range(3):
                    laplace = (
                        second_derivative(xsh(fs, c, c))
                        + second_derivative(ysh(fs, c))
                        + second_derivative(zsh(fs, c))
                    )
                    field_dy = first_derivative(ysh(fs, c))
                    rate = curl[c] + DIFFUSIVITY * laplace - sweep * field_dy
                    if c == 1:
                        rate = rate + (-STRETCH_RATE) * centre0
                    reg = r_ref[0, c, 0, pl.ds(8 * h, 8), :]
                    new_reg = RK_ALPHA * reg + TIME_STEP * rate
                    centre = fs[c, z, pl.ds(r0, 8), :]
                    nr_ref[0, c, 0, pl.ds(8 * h, 8), :] = new_reg
                    nf_ref[0, c, 0, pl.ds(8 * h, 8), :] = centre + RK_BETA * new_reg

        step(z)

    return kernel


def stencil(fi, pat, field, fb8, fa8, register, vel32, ghost, prev):
    fields, _, planes, rows, width = field.shape
    blk = lambda r: pl.BlockSpec((1, 3, planes, r, width), lambda i: (fi, 0, 0, 0, 0))
    one = lambda r: pl.BlockSpec((1, 3, planes, r, width), lambda i: (0, 0, 0, 0, 0))
    per_z = pl.BlockSpec((1, 3, 1, rows, width), lambda i: (fi, 0, i, 0, 0))
    out_sds = jax.ShapeDtypeStruct(field.shape, jnp.float32)
    in_specs = [
        pl.BlockSpec(memory_space=pltpu.SMEM),
        blk(rows),
        pl.BlockSpec(memory_space=pltpu.VMEM),
        pl.BlockSpec(memory_space=pltpu.VMEM),
        per_z,
        pl.BlockSpec(memory_space=pltpu.VMEM),
        pl.BlockSpec((1, 6, planes, rows, 128), lambda i: (fi, 0, 0, 0, 0)),
    ]
    args = [pat, field, fb8, fa8, register, vel32, ghost]
    aliases = {}
    if prev is not None:
        in_specs += [pl.BlockSpec(memory_space=pl.ANY)] * 2
        args += list(prev)
        aliases = {7: 0, 8: 1}
    return pl.pallas_call(
        make_kernel(planes, rows, width, fi, prev is not None),
        grid=(planes,),
        in_specs=in_specs,
        out_specs=[per_z, per_z],
        out_shape=[out_sds, out_sds],
        scratch_shapes=[
            pltpu.VMEM((3, planes, rows + 2 * PAD, width), jnp.float32),
            pltpu.VMEM((3, planes, rows + 2 * PAD, width), jnp.float32),
        ],
        input_output_aliases=aliases,
        cost_estimate=pl.CostEstimate(
            flops=200 * field.size // fields,
            transcendentals=0,
            bytes_accessed=16 * field.size // fields,
        ),
        compiler_params=pltpu.CompilerParams(
            dimension_semantics=("arbitrary",), vmem_limit_bytes=64000 * 1024
        ),
    )(*args)


def body(test_field, register, velocity, shear_shift):
    fields, _, planes, rows, width = test_field.shape
    tiles = lax.axis_size("tile")
    tile = lax.axis_index("tile")
    total_rows = tiles * rows
    up = [(i, (i + 1) % tiles) for i in range(tiles)]
    down = [((i + 1) % tiles, i) for i in range(tiles)]

    field_index = lax.axis_index("tf") * fields + jnp.arange(fields)
    pattern = test_pattern(field_index, planes)
    pat = pattern.reshape(fields, 3 * planes)

    halo_dt = jnp.bfloat16
    n_f = fields * 3 * planes * HALO
    n_v = 3 * velocity.shape[1] * HALO

    def halo_rows(f, sl):
        f_part = test_field[f, :, :, sl, :].astype(halo_dt).reshape(3 * planes * HALO, width)
        if f > 0:
            return f_part
        v_part = velocity[:, :, sl, :].reshape(n_v, width)
        return jnp.concatenate([f_part, v_part], axis=0)

    n_1 = 3 * planes * HALO
    got = []
    for f in range(fields):
        got_b = lax.ppermute(halo_rows(f, slice(rows - HALO, rows)), "tile", up)
        got_a = lax.ppermute(halo_rows(f, slice(0, HALO)), "tile", down)
        if f == 0:
            vb = got_b[n_1:].reshape(3, velocity.shape[1], HALO, width)
            va = got_a[n_1:].reshape(3, velocity.shape[1], HALO, width)
        got.append((got_b[:n_1], got_a[:n_1]))

    def padded(pair):
        return pair

    vext = jnp.pad(
        jnp.concatenate([vb, velocity, va], axis=2),
        ((0, 0), (0, 0), (PAD - HALO, PAD - HALO), (0, 0)),
    )
    vel32 = lax.all_gather(vext, "tf", axis=1, tiled=True)

    strip_f = jnp.concatenate([test_field[..., width - HALO :], test_field[..., :HALO]], axis=-1)
    strip_v = jnp.concatenate([velocity[..., width - HALO :], velocity[..., :HALO]], axis=-1)
    strip_v = lax.all_gather(strip_v, "tf", axis=1, tiled=True)
    strip_e = cross_emf(strip_v, (strip_f + pattern).astype(jnp.bfloat16)).astype(jnp.float32)
    comb = jnp.concatenate([strip_f, strip_e], axis=1)
    chans = HALO * fields * 6
    packed = jnp.transpose(comb, (4, 0, 1, 2, 3)).reshape(1, 2 * chans, planes * rows)
    gathered = lax.all_gather(packed, "tile", axis=0, tiled=True)
    row_of = lax.broadcasted_iota(jnp.int32, (chans, planes * rows), 1) % rows

    def select(part, shift):
        start = (tile * rows + shift) % total_rows
        first = start // rows
        offset = start % rows
        near = lax.dynamic_index_in_dim(part, first, 0, keepdims=False)
        far = lax.dynamic_index_in_dim(part, (first + 1) % tiles, 0, keepdims=False)
        near = jnp.roll(near, -offset, axis=1)
        far = jnp.roll(far, rows - offset, axis=1)
        picked = jnp.where(row_of + offset < rows, near, far)
        return picked.reshape(HALO, fields, 6, planes, rows)

    lo = select(gathered[:, :chans], shear_shift[0])
    hi = select(gathered[:, chans:], shear_shift[1])
    lane = lax.broadcasted_iota(jnp.int32, (1, 1, 1, 1, 128), 4)
    ghost = jnp.zeros((fields, 6, planes, rows, 128), jnp.float32)
    for j in range(HALO):
        ghost = jnp.where(lane == j, hi[j][..., None], ghost)
        ghost = jnp.where(lane == 128 - HALO + j, lo[j][..., None], ghost)

    prev = None
    for f in range(fields):
        pair = got[f]
        if prev is not None:
            pair, prev = lax.optimization_barrier((pair, prev))
        fb, fa = padded(pair)
        prev = stencil(f, pat, test_field, fb, fa, register, vel32, ghost, prev)
    new_field, new_register = prev
    return (new_field, new_register)


def solution(mesh):
    return jax.shard_map(
        body,
        mesh=mesh,
        in_specs=(
            P("tf", None, None, "tile", None),
            P("tf", None, None, "tile", None),
            P(None, "tf", "tile", None),
            P(),
        ),
        out_specs=(P("tf", None, None, "tile", None), P("tf", None, None, "tile", None)),
        check_vma=False,
    )
```

```python
import math

import jax
import jax.numpy as jnp
from jax import lax
from jax.experimental import pallas as pl
from jax.experimental.pallas import tpu as pltpu
from jax.sharding import PartitionSpec as P

DIFFUSIVITY = 0.1
TIME_STEP = 0.3
RK_ALPHA = -5.0 / 9.0
RK_BETA = 15.0 / 16.0
SWEEP_SPEED = 0.75
STRETCH_RATE = 0.375
HALO = 3
PAD = 8


def first_derivative(shifted):
    return (
        45.0 * (shifted(1) - shifted(-1))
        - 9.0 * (shifted(2) - shifted(-2))
        + (shifted(3) - shifted(-3))
    ) / 60.0


def second_derivative(shifted):
    return (
        -49.0 / 18.0 * shifted(0)
        + 1.5 * (shifted(1) + shifted(-1))
        - 0.15 * (shifted(2) + shifted(-2))
        + (shifted(3) + shifted(-3)) / 90.0
    )


def test_pattern(field_index, planes):
    height = jnp.arange(planes).astype(jnp.float32)
    wavenumber = (field_index // 4 + 1).astype(jnp.float32)
    phase = 2.0 * math.pi * wavenumber[:, None] * height[None, :] / planes
    profile = jnp.where((field_index // 2 % 2 == 0)[:, None], jnp.cos(phase), jnp.sin(phase))
    component = field_index % 2
    selector = (jnp.arange(3)[None, :] == component[:, None]).astype(jnp.float32)
    return (selector[:, :, None] * profile[:, None, :])[:, :, :, None, None]


def cross_emf(velocity, summed):
    vel = velocity.astype(jnp.float32)
    fld = summed.astype(jnp.float32)
    emf_x = vel[1] * fld[:, 2] - vel[2] * fld[:, 1]
    emf_y = vel[2] * fld[:, 0] - vel[0] * fld[:, 2]
    emf_z = vel[0] * fld[:, 1] - vel[1] * fld[:, 0]
    return jnp.stack([emf_x, emf_y, emf_z], 1).astype(jnp.bfloat16)


def _bf(x):
    return x.astype(jnp.bfloat16).astype(jnp.float32)


def make_kernel(planes, rows, width, fi, aliased):
    ext_w = width + 256

    def kernel(pat_ref, f_ref, fb_ref, fa_ref, r_ref, v_ref, g_ref, *rest):
        if aliased:
            rest = rest[2:]
        nf_ref, nr_ref, fs, es = rest

        def fill_halo():
            for zz in range(planes):
                for c in range(3):
                    at = (c * planes + zz) * HALO
                    got_b = fb_ref[at : at + HALO, :].astype(jnp.float32)
                    got_a = fa_ref[at : at + HALO, :].astype(jnp.float32)
                    fs[c, zz, PAD - HALO : PAD, :] = got_b
                    fs[c, zz, PAD + rows : PAD + rows + HALO, :] = got_a

        def fill(z, carry):
            for c in range(3):
                fs[c, z, PAD : PAD + rows, :] = f_ref[0, c, z]
            s = [_bf(fs[c, z] + pat_ref[fi, c * planes + z]) for c in range(3)]
            v = [v_ref[c, z].astype(jnp.float32) for c in range(3)]
            es[0, z] = _bf(v[1] * s[2] - v[2] * s[1])
            es[1, z] = _bf(v[2] * s[0] - v[0] * s[2])
            es[2, z] = _bf(v[0] * s[1] - v[1] * s[0])
            return carry

        z = pl.program_id(0)

        @pl.when(z == 0)
        def _():
            fill_halo()
            lax.fori_loop(0, planes, fill, 0)

        xpos = lax.broadcasted_iota(jnp.int32, (8, width), 1).astype(jnp.float32)
        sweep = -SWEEP_SPEED * (2.0 * xpos / (width - 1) - 1.0)

        def step(z):
            zi = {o: lax.rem(z + o + planes, planes) for o in range(-HALO, HALO + 1)}
            for h in range(rows // 8):
                r0 = PAD + 8 * h

                def ysh(buf, c):
                    return lambda o: buf[c, z, pl.ds(r0 + o, 8), :]

                def zsh(buf, c):
                    return lambda o: buf[c, zi[o], pl.ds(r0, 8), :]

                def xsh(buf, c, gch):
                    g = g_ref[0, gch, z, pl.ds(8 * h, 8), :]
                    ext = jnp.concatenate([g, buf[c, z, pl.ds(r0, 8), :], g], axis=-1)

                    def shifted(o):
                        if o == 0:
                            return buf[c, z, pl.ds(r0, 8), :]
                        return pltpu.roll(ext, (-o) % ext_w, 1)[:, 128 : 128 + width]

                    return shifted

                curl = [
                    first_derivative(ysh(es, 2)) - first_derivative(zsh(es, 1)),
                    first_derivative(zsh(es, 0)) - first_derivative(xsh(es, 2, 5)),
                    first_derivative(xsh(es, 1, 4)) - first_derivative(ysh(es, 0)),
                ]
                centre0 = fs[0, z, pl.ds(r0, 8), :]
                for c in range(3):
                    laplace = (
                        second_derivative(xsh(fs, c, c))
                        + second_derivative(ysh(fs, c))
                        + second_derivative(zsh(fs, c))
                    )
                    field_dy = first_derivative(ysh(fs, c))
                    rate = curl[c] + DIFFUSIVITY * laplace - sweep * field_dy
                    if c == 1:
                        rate = rate + (-STRETCH_RATE) * centre0
                    reg = r_ref[0, c, 0, pl.ds(8 * h, 8), :]
                    new_reg = RK_ALPHA * reg + TIME_STEP * rate
                    centre = fs[c, z, pl.ds(r0, 8), :]
                    nr_ref[0, c, 0, pl.ds(8 * h, 8), :] = new_reg
                    nf_ref[0, c, 0, pl.ds(8 * h, 8), :] = centre + RK_BETA * new_reg

        step(z)

    return kernel


def stencil(fi, pat, field, fb8, fa8, register, vel32, ghost, prev):
    fields, _, planes, rows, width = field.shape
    blk = lambda r: pl.BlockSpec((1, 3, planes, r, width), lambda i: (fi, 0, 0, 0, 0))
    one = lambda r: pl.BlockSpec((1, 3, planes, r, width), lambda i: (0, 0, 0, 0, 0))
    per_z = pl.BlockSpec((1, 3, 1, rows, width), lambda i: (fi, 0, i, 0, 0))
    out_sds = jax.ShapeDtypeStruct(field.shape, jnp.float32)
    in_specs = [
        pl.BlockSpec(memory_space=pltpu.SMEM),
        blk(rows),
        pl.BlockSpec(memory_space=pltpu.VMEM),
        pl.BlockSpec(memory_space=pltpu.VMEM),
        per_z,
        pl.BlockSpec(memory_space=pltpu.VMEM),
        pl.BlockSpec((1, 6, planes, rows, 128), lambda i: (fi, 0, 0, 0, 0)),
    ]
    args = [pat, field, fb8, fa8, register, vel32, ghost]
    aliases = {}
    if prev is not None:
        in_specs += [pl.BlockSpec(memory_space=pl.ANY)] * 2
        args += list(prev)
        aliases = {7: 0, 8: 1}
    return pl.pallas_call(
        make_kernel(planes, rows, width, fi, prev is not None),
        grid=(planes,),
        in_specs=in_specs,
        out_specs=[per_z, per_z],
        out_shape=[out_sds, out_sds],
        scratch_shapes=[
            pltpu.VMEM((3, planes, rows + 2 * PAD, width), jnp.float32),
            pltpu.VMEM((3, planes, rows + 2 * PAD, width), jnp.float32),
        ],
        input_output_aliases=aliases,
        cost_estimate=pl.CostEstimate(
            flops=200 * field.size // fields,
            transcendentals=0,
            bytes_accessed=16 * field.size // fields,
        ),
        compiler_params=pltpu.CompilerParams(
            dimension_semantics=("arbitrary",), vmem_limit_bytes=64000 * 1024
        ),
    )(*args)


def body(test_field, register, velocity, shear_shift):
    fields, _, planes, rows, width = test_field.shape
    tiles = lax.axis_size("tile")
    tile = lax.axis_index("tile")
    total_rows = tiles * rows
    up = [(i, (i + 1) % tiles) for i in range(tiles)]
    down = [((i + 1) % tiles, i) for i in range(tiles)]

    field_index = lax.axis_index("tf") * fields + jnp.arange(fields)
    pattern = test_pattern(field_index, planes)
    pat = pattern.reshape(fields, 3 * planes)

    halo_dt = jnp.bfloat16
    n_f = fields * 3 * planes * HALO
    n_v = 3 * velocity.shape[1] * HALO

    edges = lax.optimization_barrier(
        (test_field[..., rows - HALO :, :], test_field[..., :HALO, :])
    )

    def halo_rows(f, sl):
        edge = edges[0] if sl.start else edges[1]
        f_part = edge[f].astype(halo_dt).reshape(3 * planes * HALO, width)
        if f > 0:
            return f_part
        v_part = velocity[:, :, sl, :].reshape(n_v, width)
        return jnp.concatenate([f_part, v_part], axis=0)

    n_1 = 3 * planes * HALO
    got = []
    for f in range(fields):
        got_b = lax.ppermute(halo_rows(f, slice(rows - HALO, rows)), "tile", up)
        got_a = lax.ppermute(halo_rows(f, slice(0, HALO)), "tile", down)
        if f == 0:
            vb = got_b[n_1:].reshape(3, velocity.shape[1], HALO, width)
            va = got_a[n_1:].reshape(3, velocity.shape[1], HALO, width)
        got.append((got_b[:n_1], got_a[:n_1]))

    def padded(pair):
        return pair

    vext = jnp.pad(
        jnp.concatenate([vb, velocity, va], axis=2),
        ((0, 0), (0, 0), (PAD - HALO, PAD - HALO), (0, 0)),
    )
    vel32 = lax.all_gather(vext, "tf", axis=1, tiled=True)

    strip_f = jnp.concatenate([test_field[..., width - HALO :], test_field[..., :HALO]], axis=-1)
    strip_v = jnp.concatenate([velocity[..., width - HALO :], velocity[..., :HALO]], axis=-1)
    strip_v = lax.all_gather(strip_v, "tf", axis=1, tiled=True)
    strip_e = cross_emf(strip_v, (strip_f + pattern).astype(jnp.bfloat16)).astype(jnp.float32)
    comb = jnp.concatenate([strip_f, strip_e], axis=1)
    chans = HALO * fields * 6
    packed = jnp.transpose(comb, (4, 0, 1, 2, 3)).reshape(1, 2 * chans, planes * rows)
    gathered = lax.all_gather(packed, "tile", axis=0, tiled=True)
    row_of = lax.broadcasted_iota(jnp.int32, (chans, planes * rows), 1) % rows

    def select(part, shift):
        start = (tile * rows + shift) % total_rows
        first = start // rows
        offset = start % rows
        near = lax.dynamic_index_in_dim(part, first, 0, keepdims=False)
        far = lax.dynamic_index_in_dim(part, (first + 1) % tiles, 0, keepdims=False)
        near = jnp.roll(near, -offset, axis=1)
        far = jnp.roll(far, rows - offset, axis=1)
        picked = jnp.where(row_of + offset < rows, near, far)
        return picked.reshape(HALO, fields, 6, planes, rows)

    lo = select(gathered[:, :chans], shear_shift[0])
    hi = select(gathered[:, chans:], shear_shift[1])
    lane = lax.broadcasted_iota(jnp.int32, (1, 1, 1, 1, 128), 4)
    ghost = jnp.zeros((fields, 6, planes, rows, 128), jnp.float32)
    for j in range(HALO):
        ghost = jnp.where(lane == j, hi[j][..., None], ghost)
        ghost = jnp.where(lane == 128 - HALO + j, lo[j][..., None], ghost)

    prev = None
    for f in range(fields):
        pair = got[f]
        if prev is not None:
            pair, prev = lax.optimization_barrier((pair, prev))
        fb, fa = padded(pair)
        prev = stencil(f, pat, test_field, fb, fa, register, vel32, ghost, prev)
    new_field, new_register = prev
    return (new_field, new_register)


def solution(mesh):
    return jax.shard_map(
        body,
        mesh=mesh,
        in_specs=(
            P("tf", None, None, "tile", None),
            P("tf", None, None, "tile", None),
            P(None, "tf", "tile", None),
            P(),
        ),
        out_specs=(P("tf", None, None, "tile", None), P("tf", None, None, "tile", None)),
        check_vma=False,
    )
```

```python
import math

import jax
import jax.numpy as jnp
from jax import lax
from jax.experimental import pallas as pl
from jax.experimental.pallas import tpu as pltpu
from jax.sharding import PartitionSpec as P

DIFFUSIVITY = 0.1
TIME_STEP = 0.3
RK_ALPHA = -5.0 / 9.0
RK_BETA = 15.0 / 16.0
SWEEP_SPEED = 0.75
STRETCH_RATE = 0.375
HALO = 3
PAD = 8


def first_derivative(shifted):
    return (
        45.0 * (shifted(1) - shifted(-1))
        - 9.0 * (shifted(2) - shifted(-2))
        + (shifted(3) - shifted(-3))
    ) / 60.0


def second_derivative(shifted):
    return (
        -49.0 / 18.0 * shifted(0)
        + 1.5 * (shifted(1) + shifted(-1))
        - 0.15 * (shifted(2) + shifted(-2))
        + (shifted(3) + shifted(-3)) / 90.0
    )


def test_pattern(field_index, planes):
    height = jnp.arange(planes).astype(jnp.float32)
    wavenumber = (field_index // 4 + 1).astype(jnp.float32)
    phase = 2.0 * math.pi * wavenumber[:, None] * height[None, :] / planes
    profile = jnp.where((field_index // 2 % 2 == 0)[:, None], jnp.cos(phase), jnp.sin(phase))
    component = field_index % 2
    selector = (jnp.arange(3)[None, :] == component[:, None]).astype(jnp.float32)
    return (selector[:, :, None] * profile[:, None, :])[:, :, :, None, None]


def cross_emf(velocity, summed):
    vel = velocity.astype(jnp.float32)
    fld = summed.astype(jnp.float32)
    emf_x = vel[1] * fld[:, 2] - vel[2] * fld[:, 1]
    emf_y = vel[2] * fld[:, 0] - vel[0] * fld[:, 2]
    emf_z = vel[0] * fld[:, 1] - vel[1] * fld[:, 0]
    return jnp.stack([emf_x, emf_y, emf_z], 1).astype(jnp.bfloat16)


def _bf(x):
    return x.astype(jnp.bfloat16).astype(jnp.float32)


def make_kernel(planes, rows, width, fi, aliased):
    ext_w = width + 256

    def kernel(pat_ref, f_ref, fb_ref, fa_ref, r_ref, v_ref, g_ref, *rest):
        if aliased:
            rest = rest[2:]
        nf_ref, nr_ref, fs, es = rest

        def fill_halo():
            for zz in range(planes):
                for c in range(3):
                    at = (c * planes + zz) * HALO
                    got_b = fb_ref[at : at + HALO, :].astype(jnp.float32)
                    got_a = fa_ref[at : at + HALO, :].astype(jnp.float32)
                    fs[c, zz, PAD - HALO : PAD, :] = got_b
                    fs[c, zz, PAD + rows : PAD + rows + HALO, :] = got_a

        def fill(z, carry):
            for c in range(3):
                fs[c, z, PAD : PAD + rows, :] = f_ref[0, c, z]
            s = [_bf(fs[c, z] + pat_ref[fi, c * planes + z]) for c in range(3)]
            v = [v_ref[c, z].astype(jnp.float32) for c in range(3)]
            es[0, z] = _bf(v[1] * s[2] - v[2] * s[1])
            es[1, z] = _bf(v[2] * s[0] - v[0] * s[2])
            es[2, z] = _bf(v[0] * s[1] - v[1] * s[0])
            return carry

        z = pl.program_id(0)

        @pl.when(z == 0)
        def _():
            fill_halo()
            lax.fori_loop(0, planes, fill, 0)

        xpos = lax.broadcasted_iota(jnp.int32, (8, width), 1).astype(jnp.float32)
        sweep = -SWEEP_SPEED * (2.0 * xpos / (width - 1) - 1.0)

        def step(z):
            zi = {o: lax.rem(z + o + planes, planes) for o in range(-HALO, HALO + 1)}
            for h in range(rows // 8):
                r0 = PAD + 8 * h

                def ysh(buf, c):
                    return lambda o: buf[c, z, pl.ds(r0 + o, 8), :]

                def zsh(buf, c):
                    return lambda o: buf[c, zi[o], pl.ds(r0, 8), :]

                def xsh(buf, c, gch):
                    g = g_ref[0, gch, z, pl.ds(8 * h, 8), :]
                    ext = jnp.concatenate([g, buf[c, z, pl.ds(r0, 8), :], g], axis=-1)

                    def shifted(o):
                        if o == 0:
                            return buf[c, z, pl.ds(r0, 8), :]
                        return pltpu.roll(ext, (-o) % ext_w, 1)[:, 128 : 128 + width]

                    return shifted

                curl = [
                    first_derivative(ysh(es, 2)) - first_derivative(zsh(es, 1)),
                    first_derivative(zsh(es, 0)) - first_derivative(xsh(es, 2, 5)),
                    first_derivative(xsh(es, 1, 4)) - first_derivative(ysh(es, 0)),
                ]
                centre0 = fs[0, z, pl.ds(r0, 8), :]
                for c in range(3):
                    laplace = (
                        second_derivative(xsh(fs, c, c))
                        + second_derivative(ysh(fs, c))
                        + second_derivative(zsh(fs, c))
                    )
                    field_dy = first_derivative(ysh(fs, c))
                    rate = curl[c] + DIFFUSIVITY * laplace - sweep * field_dy
                    if c == 1:
                        rate = rate + (-STRETCH_RATE) * centre0
                    reg = r_ref[0, c, 0, pl.ds(8 * h, 8), :]
                    new_reg = RK_ALPHA * reg + TIME_STEP * rate
                    centre = fs[c, z, pl.ds(r0, 8), :]
                    nr_ref[0, c, 0, pl.ds(8 * h, 8), :] = new_reg
                    nf_ref[0, c, 0, pl.ds(8 * h, 8), :] = centre + RK_BETA * new_reg

        step(z)

    return kernel


def stencil(fi, pat, field, fb8, fa8, register, vel32, ghost, prev):
    fields, _, planes, rows, width = field.shape
    blk = lambda r: pl.BlockSpec((1, 3, planes, r, width), lambda i: (fi, 0, 0, 0, 0))
    one = lambda r: pl.BlockSpec((1, 3, planes, r, width), lambda i: (0, 0, 0, 0, 0))
    per_z = pl.BlockSpec((1, 3, 1, rows, width), lambda i: (fi, 0, i, 0, 0))
    out_sds = jax.ShapeDtypeStruct(field.shape, jnp.float32)
    in_specs = [
        pl.BlockSpec(memory_space=pltpu.SMEM),
        blk(rows),
        pl.BlockSpec(memory_space=pltpu.VMEM),
        pl.BlockSpec(memory_space=pltpu.VMEM),
        per_z,
        pl.BlockSpec(memory_space=pltpu.VMEM),
        pl.BlockSpec((1, 6, planes, rows, 128), lambda i: (fi, 0, 0, 0, 0)),
    ]
    args = [pat, field, fb8, fa8, register, vel32, ghost]
    aliases = {}
    if prev is not None:
        in_specs += [pl.BlockSpec(memory_space=pl.ANY)] * 2
        args += list(prev)
        aliases = {7: 0, 8: 1}
    return pl.pallas_call(
        make_kernel(planes, rows, width, fi, prev is not None),
        grid=(planes,),
        in_specs=in_specs,
        out_specs=[per_z, per_z],
        out_shape=[out_sds, out_sds],
        scratch_shapes=[
            pltpu.VMEM((3, planes, rows + 2 * PAD, width), jnp.float32),
            pltpu.VMEM((3, planes, rows + 2 * PAD, width), jnp.float32),
        ],
        input_output_aliases=aliases,
        cost_estimate=pl.CostEstimate(
            flops=200 * field.size // fields,
            transcendentals=0,
            bytes_accessed=16 * field.size // fields,
        ),
        compiler_params=pltpu.CompilerParams(
            dimension_semantics=("arbitrary",), vmem_limit_bytes=64000 * 1024
        ),
    )(*args)


def body(test_field, register, velocity, shear_shift):
    fields, _, planes, rows, width = test_field.shape
    tiles = lax.axis_size("tile")
    tile = lax.axis_index("tile")
    total_rows = tiles * rows
    up = [(i, (i + 1) % tiles) for i in range(tiles)]
    down = [((i + 1) % tiles, i) for i in range(tiles)]

    field_index = lax.axis_index("tf") * fields + jnp.arange(fields)
    pattern = test_pattern(field_index, planes)
    pat = pattern.reshape(fields, 3 * planes)

    halo_dt = jnp.bfloat16
    n_f = fields * 3 * planes * HALO
    n_v = 3 * velocity.shape[1] * HALO

    edges = lax.optimization_barrier(
        (test_field[..., rows - HALO :, :], test_field[..., :HALO, :])
    )

    def halo_rows(f, sl):
        edge = edges[0] if sl.start else edges[1]
        f_part = edge[f].astype(halo_dt).reshape(3 * planes * HALO, width)
        if f > 0:
            return f_part
        v_part = velocity[:, :, sl, :].reshape(n_v, width)
        return jnp.concatenate([f_part, v_part], axis=0)

    n_1 = 3 * planes * HALO
    got = []
    for f in range(fields):
        got_b = lax.ppermute(halo_rows(f, slice(rows - HALO, rows)), "tile", up)
        got_a = lax.ppermute(halo_rows(f, slice(0, HALO)), "tile", down)
        if f == 0:
            vb = got_b[n_1:].reshape(3, velocity.shape[1], HALO, width)
            va = got_a[n_1:].reshape(3, velocity.shape[1], HALO, width)
        got.append((got_b[:n_1], got_a[:n_1]))

    def padded(pair):
        return pair

    vext = jnp.pad(
        jnp.concatenate([vb, velocity, va], axis=2),
        ((0, 0), (0, 0), (PAD - HALO, PAD - HALO), (0, 0)),
    )
    groups = lax.axis_size("tf")
    me = lax.axis_index("tf")
    held = [vext]
    for k in range(1, groups):
        pairs = [(i, (i + k) % groups) for i in range(groups)]
        held.append(lax.ppermute(vext, "tf", pairs))
    held = jnp.stack(held, 0)
    order = (me - jnp.arange(groups)) % groups
    vel32 = jnp.take(held, order, axis=0)
    vel32 = jnp.moveaxis(vel32, 0, 1).reshape(3, planes, vext.shape[2], width)

    strip_f = jnp.concatenate([test_field[..., width - HALO :], test_field[..., :HALO]], axis=-1)
    strip_v = jnp.concatenate([velocity[..., width - HALO :], velocity[..., :HALO]], axis=-1)
    strip_v = lax.all_gather(strip_v, "tf", axis=1, tiled=True)
    strip_e = cross_emf(strip_v, (strip_f + pattern).astype(jnp.bfloat16)).astype(jnp.float32)
    comb = jnp.concatenate([strip_f, strip_e], axis=1)
    chans = HALO * fields * 6
    packed = jnp.transpose(comb, (4, 0, 1, 2, 3)).reshape(1, 2 * chans, planes * rows)
    gathered = lax.all_gather(packed, "tile", axis=0, tiled=True)
    row_of = lax.broadcasted_iota(jnp.int32, (chans, planes * rows), 1) % rows

    def select(part, shift):
        start = (tile * rows + shift) % total_rows
        first = start // rows
        offset = start % rows
        near = lax.dynamic_index_in_dim(part, first, 0, keepdims=False)
        far = lax.dynamic_index_in_dim(part, (first + 1) % tiles, 0, keepdims=False)
        near = jnp.roll(near, -offset, axis=1)
        far = jnp.roll(far, rows - offset, axis=1)
        picked = jnp.where(row_of + offset < rows, near, far)
        return picked.reshape(HALO, fields, 6, planes, rows)

    lo = select(gathered[:, :chans], shear_shift[0])
    hi = select(gathered[:, chans:], shear_shift[1])
    lane = lax.broadcasted_iota(jnp.int32, (1, 1, 1, 1, 128), 4)
    ghost = jnp.zeros((fields, 6, planes, rows, 128), jnp.float32)
    for j in range(HALO):
        ghost = jnp.where(lane == j, hi[j][..., None], ghost)
        ghost = jnp.where(lane == 128 - HALO + j, lo[j][..., None], ghost)

    prev = None
    for f in range(fields):
        pair = got[f]
        if prev is not None:
            pair, prev = lax.optimization_barrier((pair, prev))
        fb, fa = padded(pair)
        prev = stencil(f, pat, test_field, fb, fa, register, vel32, ghost, prev)
    new_field, new_register = prev
    return (new_field, new_register)


def solution(mesh):
    return jax.shard_map(
        body,
        mesh=mesh,
        in_specs=(
            P("tf", None, None, "tile", None),
            P("tf", None, None, "tile", None),
            P(None, "tf", "tile", None),
            P(),
        ),
        out_specs=(P("tf", None, None, "tile", None), P("tf", None, None, "tile", None)),
        check_vma=False,
    )
```

```python
import math

import jax
import jax.numpy as jnp
from jax import lax
from jax.experimental import pallas as pl
from jax.experimental.pallas import tpu as pltpu
from jax.sharding import PartitionSpec as P

DIFFUSIVITY = 0.1
TIME_STEP = 0.3
RK_ALPHA = -5.0 / 9.0
RK_BETA = 15.0 / 16.0
SWEEP_SPEED = 0.75
STRETCH_RATE = 0.375
HALO = 3
PAD = 8


def first_derivative(shifted):
    return (
        45.0 * (shifted(1) - shifted(-1))
        - 9.0 * (shifted(2) - shifted(-2))
        + (shifted(3) - shifted(-3))
    ) / 60.0


def second_derivative(shifted):
    return (
        -49.0 / 18.0 * shifted(0)
        + 1.5 * (shifted(1) + shifted(-1))
        - 0.15 * (shifted(2) + shifted(-2))
        + (shifted(3) + shifted(-3)) / 90.0
    )


def test_pattern(field_index, planes):
    height = jnp.arange(planes).astype(jnp.float32)
    wavenumber = (field_index // 4 + 1).astype(jnp.float32)
    phase = 2.0 * math.pi * wavenumber[:, None] * height[None, :] / planes
    profile = jnp.where((field_index // 2 % 2 == 0)[:, None], jnp.cos(phase), jnp.sin(phase))
    component = field_index % 2
    selector = (jnp.arange(3)[None, :] == component[:, None]).astype(jnp.float32)
    return (selector[:, :, None] * profile[:, None, :])[:, :, :, None, None]


def cross_emf(velocity, summed):
    vel = velocity.astype(jnp.float32)
    fld = summed.astype(jnp.float32)
    emf_x = vel[1] * fld[:, 2] - vel[2] * fld[:, 1]
    emf_y = vel[2] * fld[:, 0] - vel[0] * fld[:, 2]
    emf_z = vel[0] * fld[:, 1] - vel[1] * fld[:, 0]
    return jnp.stack([emf_x, emf_y, emf_z], 1).astype(jnp.bfloat16)


def _bf(x):
    return x.astype(jnp.bfloat16).astype(jnp.float32)


def make_kernel(planes, rows, width, fi, aliased):
    ext_w = width + 256

    def kernel(pat_ref, f_ref, fb_ref, fa_ref, r_ref, v_ref, g_ref, *rest):
        if aliased:
            rest = rest[2:]
        nf_ref, nr_ref, fs, es = rest

        def fill_halo():
            for zz in range(planes):
                for c in range(3):
                    at = (c * planes + zz) * HALO
                    got_b = fb_ref[at : at + HALO, :].astype(jnp.float32)
                    got_a = fa_ref[at : at + HALO, :].astype(jnp.float32)
                    fs[c, zz, PAD - HALO : PAD, :] = got_b
                    fs[c, zz, PAD + rows : PAD + rows + HALO, :] = got_a

        def fill(z, carry):
            for c in range(3):
                fs[c, z, PAD : PAD + rows, :] = f_ref[0, c, z]
            s = [_bf(fs[c, z] + pat_ref[fi, c * planes + z]) for c in range(3)]
            v = [v_ref[c, z].astype(jnp.float32) for c in range(3)]
            es[0, z] = _bf(v[1] * s[2] - v[2] * s[1])
            es[1, z] = _bf(v[2] * s[0] - v[0] * s[2])
            es[2, z] = _bf(v[0] * s[1] - v[1] * s[0])
            return carry

        z = pl.program_id(0)

        @pl.when(z == 0)
        def _():
            fill_halo()
            lax.fori_loop(0, planes, fill, 0)

        xpos = lax.broadcasted_iota(jnp.int32, (8, width), 1).astype(jnp.float32)
        lane = lax.broadcasted_iota(jnp.int32, (8, 128), 1)
        sweep = -SWEEP_SPEED * (2.0 * xpos / (width - 1) - 1.0)

        def step(z):
            zi = {o: lax.rem(z + o + planes, planes) for o in range(-HALO, HALO + 1)}
            for h in range(rows // 8):
                r0 = PAD + 8 * h

                def ysh(buf, c):
                    return lambda o: buf[c, z, pl.ds(r0 + o, 8), :]

                def zsh(buf, c):
                    return lambda o: buf[c, zi[o], pl.ds(r0, 8), :]

                def xsh(buf, c, gch):
                    g = g_ref[0, gch, z, pl.ds(8 * h, 8), :]
                    centre = buf[c, z, pl.ds(r0, 8), :]

                    def shifted(o):
                        if o == 0:
                            return centre
                        rolled = pltpu.roll(centre, (-o) % width, 1)
                        wrapped = pltpu.roll(g, (-o) % 128, 1)
                        if o > 0:
                            edge = jnp.where(lane >= 128 - o, wrapped, rolled[:, width - 128 :])
                            return jnp.concatenate([rolled[:, : width - 128], edge], axis=-1)
                        edge = jnp.where(lane < -o, wrapped, rolled[:, :128])
                        return jnp.concatenate([edge, rolled[:, 128:]], axis=-1)

                    return shifted

                curl = [
                    first_derivative(ysh(es, 2)) - first_derivative(zsh(es, 1)),
                    first_derivative(zsh(es, 0)) - first_derivative(xsh(es, 2, 5)),
                    first_derivative(xsh(es, 1, 4)) - first_derivative(ysh(es, 0)),
                ]
                centre0 = fs[0, z, pl.ds(r0, 8), :]
                for c in range(3):
                    laplace = (
                        second_derivative(xsh(fs, c, c))
                        + second_derivative(ysh(fs, c))
                        + second_derivative(zsh(fs, c))
                    )
                    field_dy = first_derivative(ysh(fs, c))
                    rate = curl[c] + DIFFUSIVITY * laplace - sweep * field_dy
                    if c == 1:
                        rate = rate + (-STRETCH_RATE) * centre0
                    reg = r_ref[0, c, 0, pl.ds(8 * h, 8), :]
                    new_reg = RK_ALPHA * reg + TIME_STEP * rate
                    centre = fs[c, z, pl.ds(r0, 8), :]
                    nr_ref[0, c, 0, pl.ds(8 * h, 8), :] = new_reg
                    nf_ref[0, c, 0, pl.ds(8 * h, 8), :] = centre + RK_BETA * new_reg

        step(z)

    return kernel


def stencil(fi, pat, field, fb8, fa8, register, vel32, ghost, prev):
    fields, _, planes, rows, width = field.shape
    blk = lambda r: pl.BlockSpec((1, 3, planes, r, width), lambda i: (fi, 0, 0, 0, 0))
    one = lambda r: pl.BlockSpec((1, 3, planes, r, width), lambda i: (0, 0, 0, 0, 0))
    per_z = pl.BlockSpec((1, 3, 1, rows, width), lambda i: (fi, 0, i, 0, 0))
    out_sds = jax.ShapeDtypeStruct(field.shape, jnp.float32)
    in_specs = [
        pl.BlockSpec(memory_space=pltpu.SMEM),
        blk(rows),
        pl.BlockSpec(memory_space=pltpu.VMEM),
        pl.BlockSpec(memory_space=pltpu.VMEM),
        per_z,
        pl.BlockSpec(memory_space=pltpu.VMEM),
        pl.BlockSpec((1, 6, planes, rows, 128), lambda i: (fi, 0, 0, 0, 0)),
    ]
    args = [pat, field, fb8, fa8, register, vel32, ghost]
    aliases = {}
    if prev is not None:
        in_specs += [pl.BlockSpec(memory_space=pl.ANY)] * 2
        args += list(prev)
        aliases = {7: 0, 8: 1}
    return pl.pallas_call(
        make_kernel(planes, rows, width, fi, prev is not None),
        grid=(planes,),
        in_specs=in_specs,
        out_specs=[per_z, per_z],
        out_shape=[out_sds, out_sds],
        scratch_shapes=[
            pltpu.VMEM((3, planes, rows + 2 * PAD, width), jnp.float32),
            pltpu.VMEM((3, planes, rows + 2 * PAD, width), jnp.float32),
        ],
        input_output_aliases=aliases,
        cost_estimate=pl.CostEstimate(
            flops=200 * field.size // fields,
            transcendentals=0,
            bytes_accessed=16 * field.size // fields,
        ),
        compiler_params=pltpu.CompilerParams(
            dimension_semantics=("arbitrary",), vmem_limit_bytes=64000 * 1024
        ),
    )(*args)


def body(test_field, register, velocity, shear_shift):
    fields, _, planes, rows, width = test_field.shape
    tiles = lax.axis_size("tile")
    tile = lax.axis_index("tile")
    total_rows = tiles * rows
    up = [(i, (i + 1) % tiles) for i in range(tiles)]
    down = [((i + 1) % tiles, i) for i in range(tiles)]

    field_index = lax.axis_index("tf") * fields + jnp.arange(fields)
    pattern = test_pattern(field_index, planes)
    pat = pattern.reshape(fields, 3 * planes)

    halo_dt = jnp.bfloat16
    n_f = fields * 3 * planes * HALO
    n_v = 3 * velocity.shape[1] * HALO

    edges = lax.optimization_barrier(
        (test_field[..., rows - HALO :, :], test_field[..., :HALO, :])
    )

    def halo_rows(f, sl):
        edge = edges[0] if sl.start else edges[1]
        f_part = edge[f].astype(halo_dt).reshape(3 * planes * HALO, width)
        if f > 0:
            return f_part
        v_part = velocity[:, :, sl, :].reshape(n_v, width)
        return jnp.concatenate([f_part, v_part], axis=0)

    n_1 = 3 * planes * HALO
    got = []
    for f in range(fields):
        got_b = lax.ppermute(halo_rows(f, slice(rows - HALO, rows)), "tile", up)
        got_a = lax.ppermute(halo_rows(f, slice(0, HALO)), "tile", down)
        if f == 0:
            vb = got_b[n_1:].reshape(3, velocity.shape[1], HALO, width)
            va = got_a[n_1:].reshape(3, velocity.shape[1], HALO, width)
        got.append((got_b[:n_1], got_a[:n_1]))

    def padded(pair):
        return pair

    vext = jnp.pad(
        jnp.concatenate([vb, velocity, va], axis=2),
        ((0, 0), (0, 0), (PAD - HALO, PAD - HALO), (0, 0)),
    )
    vel32 = lax.all_gather(vext, "tf", axis=1, tiled=True)

    strip_f = jnp.concatenate([test_field[..., width - HALO :], test_field[..., :HALO]], axis=-1)
    strip_v = jnp.concatenate([velocity[..., width - HALO :], velocity[..., :HALO]], axis=-1)
    strip_v = lax.all_gather(strip_v, "tf", axis=1, tiled=True)
    strip_e = cross_emf(strip_v, (strip_f + pattern).astype(jnp.bfloat16)).astype(jnp.float32)
    comb = jnp.concatenate([strip_f, strip_e], axis=1)
    chans = HALO * fields * 6
    packed = jnp.transpose(comb, (4, 0, 1, 2, 3)).reshape(1, 2 * chans, planes * rows)
    gathered = lax.all_gather(packed, "tile", axis=0, tiled=True)
    row_of = lax.broadcasted_iota(jnp.int32, (chans, planes * rows), 1) % rows

    def select(part, shift):
        start = (tile * rows + shift) % total_rows
        first = start // rows
        offset = start % rows
        near = lax.dynamic_index_in_dim(part, first, 0, keepdims=False)
        far = lax.dynamic_index_in_dim(part, (first + 1) % tiles, 0, keepdims=False)
        near = jnp.roll(near, -offset, axis=1)
        far = jnp.roll(far, rows - offset, axis=1)
        picked = jnp.where(row_of + offset < rows, near, far)
        return picked.reshape(HALO, fields, 6, planes, rows)

    lo = select(gathered[:, :chans], shear_shift[0])
    hi = select(gathered[:, chans:], shear_shift[1])
    lane = lax.broadcasted_iota(jnp.int32, (1, 1, 1, 1, 128), 4)
    ghost = jnp.zeros((fields, 6, planes, rows, 128), jnp.float32)
    for j in range(HALO):
        ghost = jnp.where(lane == j, hi[j][..., None], ghost)
        ghost = jnp.where(lane == 128 - HALO + j, lo[j][..., None], ghost)

    prev = None
    for f in range(fields):
        pair = got[f]
        if prev is not None:
            pair, prev = lax.optimization_barrier((pair, prev))
        fb, fa = padded(pair)
        prev = stencil(f, pat, test_field, fb, fa, register, vel32, ghost, prev)
    new_field, new_register = prev
    return (new_field, new_register)


def solution(mesh):
    return jax.shard_map(
        body,
        mesh=mesh,
        in_specs=(
            P("tf", None, None, "tile", None),
            P("tf", None, None, "tile", None),
            P(None, "tf", "tile", None),
            P(),
        ),
        out_specs=(P("tf", None, None, "tile", None), P("tf", None, None, "tile", None)),
        check_vma=False,
    )
```

```python
import math

import jax
import jax.numpy as jnp
from jax import lax
from jax.experimental import pallas as pl
from jax.experimental.pallas import tpu as pltpu
from jax.sharding import PartitionSpec as P

DIFFUSIVITY = 0.1
TIME_STEP = 0.3
RK_ALPHA = -5.0 / 9.0
RK_BETA = 15.0 / 16.0
SWEEP_SPEED = 0.75
STRETCH_RATE = 0.375
HALO = 3
PAD = 8


def first_derivative(shifted):
    return (
        45.0 * (shifted(1) - shifted(-1))
        - 9.0 * (shifted(2) - shifted(-2))
        + (shifted(3) - shifted(-3))
    ) / 60.0


def second_derivative(shifted):
    return (
        -49.0 / 18.0 * shifted(0)
        + 1.5 * (shifted(1) + shifted(-1))
        - 0.15 * (shifted(2) + shifted(-2))
        + (shifted(3) + shifted(-3)) / 90.0
    )


def test_pattern(field_index, planes):
    height = jnp.arange(planes).astype(jnp.float32)
    wavenumber = (field_index // 4 + 1).astype(jnp.float32)
    phase = 2.0 * math.pi * wavenumber[:, None] * height[None, :] / planes
    profile = jnp.where((field_index // 2 % 2 == 0)[:, None], jnp.cos(phase), jnp.sin(phase))
    component = field_index % 2
    selector = (jnp.arange(3)[None, :] == component[:, None]).astype(jnp.float32)
    return (selector[:, :, None] * profile[:, None, :])[:, :, :, None, None]


def cross_emf(velocity, summed):
    vel = velocity.astype(jnp.float32)
    fld = summed.astype(jnp.float32)
    emf_x = vel[1] * fld[:, 2] - vel[2] * fld[:, 1]
    emf_y = vel[2] * fld[:, 0] - vel[0] * fld[:, 2]
    emf_z = vel[0] * fld[:, 1] - vel[1] * fld[:, 0]
    return jnp.stack([emf_x, emf_y, emf_z], 1).astype(jnp.bfloat16)


def _bf(x):
    return x.astype(jnp.bfloat16).astype(jnp.float32)


def make_kernel(planes, rows, width, fi, aliased):
    ext_w = width + 256

    def kernel(pat_ref, f_ref, fb_ref, fa_ref, r_ref, v_ref, g_ref, *rest):
        if aliased:
            rest = rest[2:]
        nf_ref, nr_ref, fs, es = rest

        def fill_halo():
            for zz in range(planes):
                for c in range(3):
                    at = (c * planes + zz) * HALO
                    got_b = fb_ref[at : at + HALO, :].astype(jnp.float32)
                    got_a = fa_ref[at : at + HALO, :].astype(jnp.float32)
                    fs[c, zz, PAD - HALO : PAD, :] = got_b
                    fs[c, zz, PAD + rows : PAD + rows + HALO, :] = got_a

        def fill(z, carry):
            for c in range(3):
                fs[c, z, PAD : PAD + rows, :] = f_ref[0, c, z]
            s = [_bf(fs[c, z] + pat_ref[fi, c * planes + z]) for c in range(3)]
            v = [v_ref[c, z].astype(jnp.float32) for c in range(3)]
            es[0, z] = _bf(v[1] * s[2] - v[2] * s[1])
            es[1, z] = _bf(v[2] * s[0] - v[0] * s[2])
            es[2, z] = _bf(v[0] * s[1] - v[1] * s[0])
            return carry

        z = pl.program_id(0)

        @pl.when(z == 0)
        def _():
            fill_halo()
            lax.fori_loop(0, planes, fill, 0)

        xpos = lax.broadcasted_iota(jnp.int32, (8, width), 1).astype(jnp.float32)
        sweep = -SWEEP_SPEED * (2.0 * xpos / (width - 1) - 1.0)

        def step(z):
            zi = {o: lax.rem(z + o + planes, planes) for o in range(-HALO, HALO + 1)}
            for h in range(rows // 8):
                r0 = PAD + 8 * h

                def ysh(buf, c):
                    return lambda o: buf[c, z, pl.ds(r0 + o, 8), :]

                def zsh(buf, c):
                    return lambda o: buf[c, zi[o], pl.ds(r0, 8), :]

                def xsh(buf, c, gch):
                    g = g_ref[0, gch, z, pl.ds(8 * h, 8), :]
                    ext = jnp.concatenate([g, buf[c, z, pl.ds(r0, 8), :], g], axis=-1)

                    def shifted(o):
                        if o == 0:
                            return buf[c, z, pl.ds(r0, 8), :]
                        return pltpu.roll(ext, (-o) % ext_w, 1)[:, 128 : 128 + width]

                    return shifted

                curl = [
                    first_derivative(ysh(es, 2)) - first_derivative(zsh(es, 1)),
                    first_derivative(zsh(es, 0)) - first_derivative(xsh(es, 2, 5)),
                    first_derivative(xsh(es, 1, 4)) - first_derivative(ysh(es, 0)),
                ]
                centre0 = fs[0, z, pl.ds(r0, 8), :]
                for c in range(3):
                    laplace = (
                        second_derivative(xsh(fs, c, c))
                        + second_derivative(ysh(fs, c))
                        + second_derivative(zsh(fs, c))
                    )
                    field_dy = first_derivative(ysh(fs, c))
                    rate = curl[c] + DIFFUSIVITY * laplace - sweep * field_dy
                    if c == 1:
                        rate = rate + (-STRETCH_RATE) * centre0
                    reg = r_ref[0, c, 0, pl.ds(8 * h, 8), :]
                    new_reg = RK_ALPHA * reg + TIME_STEP * rate
                    centre = fs[c, z, pl.ds(r0, 8), :]
                    nr_ref[0, c, 0, pl.ds(8 * h, 8), :] = new_reg
                    nf_ref[0, c, 0, pl.ds(8 * h, 8), :] = centre + RK_BETA * new_reg

        step(z)

    return kernel


def stencil(fi, pat, field, fb8, fa8, register, vel32, ghost, prev):
    fields, _, planes, rows, width = field.shape
    blk = lambda r: pl.BlockSpec((1, 3, planes, r, width), lambda i: (fi, 0, 0, 0, 0))
    one = lambda r: pl.BlockSpec((1, 3, planes, r, width), lambda i: (0, 0, 0, 0, 0))
    per_z = pl.BlockSpec((1, 3, 1, rows, width), lambda i: (fi, 0, i, 0, 0))
    out_sds = jax.ShapeDtypeStruct(field.shape, jnp.float32)
    in_specs = [
        pl.BlockSpec(memory_space=pltpu.SMEM),
        blk(rows),
        pl.BlockSpec(memory_space=pltpu.VMEM),
        pl.BlockSpec(memory_space=pltpu.VMEM),
        per_z,
        pl.BlockSpec(memory_space=pltpu.VMEM),
        pl.BlockSpec((1, 6, planes, rows, 128), lambda i: (fi, 0, 0, 0, 0)),
    ]
    args = [pat, field, fb8, fa8, register, vel32, ghost]
    aliases = {}
    if prev is not None:
        in_specs += [pl.BlockSpec(memory_space=pl.ANY)] * 2
        args += list(prev)
        aliases = {7: 0, 8: 1}
    return pl.pallas_call(
        make_kernel(planes, rows, width, fi, prev is not None),
        grid=(planes,),
        in_specs=in_specs,
        out_specs=[per_z, per_z],
        out_shape=[out_sds, out_sds],
        scratch_shapes=[
            pltpu.VMEM((3, planes, rows + 2 * PAD, width), jnp.float32),
            pltpu.VMEM((3, planes, rows + 2 * PAD, width), jnp.float32),
        ],
        input_output_aliases=aliases,
        cost_estimate=pl.CostEstimate(
            flops=200 * field.size // fields,
            transcendentals=0,
            bytes_accessed=16 * field.size // fields,
        ),
        compiler_params=pltpu.CompilerParams(
            dimension_semantics=("arbitrary",), vmem_limit_bytes=64000 * 1024
        ),
    )(*args)


def body(test_field, register, velocity, shear_shift):
    fields, _, planes, rows, width = test_field.shape
    tiles = lax.axis_size("tile")
    tile = lax.axis_index("tile")
    total_rows = tiles * rows
    up = [(i, (i + 1) % tiles) for i in range(tiles)]
    down = [((i + 1) % tiles, i) for i in range(tiles)]

    field_index = lax.axis_index("tf") * fields + jnp.arange(fields)
    pattern = test_pattern(field_index, planes)
    pat = pattern.reshape(fields, 3 * planes)

    halo_dt = jnp.bfloat16
    n_f = fields * 3 * planes * HALO
    n_v = 3 * velocity.shape[1] * HALO

    edges = lax.optimization_barrier(
        (test_field[..., rows - HALO :, :], test_field[..., :HALO, :])
    )

    def halo_rows(f, sl):
        edge = edges[0] if sl.start else edges[1]
        f_part = edge[f].astype(halo_dt).reshape(3 * planes * HALO, width)
        if f > 0:
            return f_part
        v_part = velocity[:, :, sl, :].reshape(n_v, width)
        return jnp.concatenate([f_part, v_part], axis=0)

    n_1 = 3 * planes * HALO
    got = []
    for f in range(fields):
        got_b = lax.ppermute(halo_rows(f, slice(rows - HALO, rows)), "tile", up)
        got_a = lax.ppermute(halo_rows(f, slice(0, HALO)), "tile", down)
        if f == 0:
            vb = got_b[n_1:].reshape(3, velocity.shape[1], HALO, width)
            va = got_a[n_1:].reshape(3, velocity.shape[1], HALO, width)
        got.append((got_b[:n_1], got_a[:n_1]))

    def padded(pair):
        return pair

    vext = jnp.concatenate([vb, velocity, va], axis=2)
    vel32 = jnp.pad(
        lax.all_gather(vext, "tf", axis=1, tiled=True),
        ((0, 0), (0, 0), (PAD - HALO, PAD - HALO), (0, 0)),
    )

    strip_f = jnp.concatenate([test_field[..., width - HALO :], test_field[..., :HALO]], axis=-1)
    strip_v = jnp.concatenate([velocity[..., width - HALO :], velocity[..., :HALO]], axis=-1)
    strip_v = lax.all_gather(strip_v, "tf", axis=1, tiled=True)
    strip_e = cross_emf(strip_v, (strip_f + pattern).astype(jnp.bfloat16)).astype(jnp.float32)
    comb = jnp.concatenate([strip_f, strip_e], axis=1)
    chans = HALO * fields * 6
    packed = jnp.transpose(comb, (4, 0, 1, 2, 3)).reshape(1, 2 * chans, planes * rows)
    gathered = lax.all_gather(packed, "tile", axis=0, tiled=True)
    row_of = lax.broadcasted_iota(jnp.int32, (chans, planes * rows), 1) % rows

    def select(part, shift):
        start = (tile * rows + shift) % total_rows
        first = start // rows
        offset = start % rows
        near = lax.dynamic_index_in_dim(part, first, 0, keepdims=False)
        far = lax.dynamic_index_in_dim(part, (first + 1) % tiles, 0, keepdims=False)
        near = jnp.roll(near, -offset, axis=1)
        far = jnp.roll(far, rows - offset, axis=1)
        picked = jnp.where(row_of + offset < rows, near, far)
        return picked.reshape(HALO, fields, 6, planes, rows)

    lo = select(gathered[:, :chans], shear_shift[0])
    hi = select(gathered[:, chans:], shear_shift[1])
    lane = lax.broadcasted_iota(jnp.int32, (1, 1, 1, 1, 128), 4)
    ghost = jnp.zeros((fields, 6, planes, rows, 128), jnp.float32)
    for j in range(HALO):
        ghost = jnp.where(lane == j, hi[j][..., None], ghost)
        ghost = jnp.where(lane == 128 - HALO + j, lo[j][..., None], ghost)

    prev = None
    for f in range(fields):
        pair = got[f]
        if prev is not None:
            pair, prev = lax.optimization_barrier((pair, prev))
        fb, fa = padded(pair)
        prev = stencil(f, pat, test_field, fb, fa, register, vel32, ghost, prev)
    new_field, new_register = prev
    return (new_field, new_register)


def solution(mesh):
    return jax.shard_map(
        body,
        mesh=mesh,
        in_specs=(
            P("tf", None, None, "tile", None),
            P("tf", None, None, "tile", None),
            P(None, "tf", "tile", None),
            P(),
        ),
        out_specs=(P("tf", None, None, "tile", None), P("tf", None, None, "tile", None)),
        check_vma=False,
    )
```

```python
import math

import jax
import jax.numpy as jnp
from jax import lax
from jax.experimental import pallas as pl
from jax.experimental.pallas import tpu as pltpu
from jax.sharding import PartitionSpec as P

DIFFUSIVITY = 0.1
TIME_STEP = 0.3
RK_ALPHA = -5.0 / 9.0
RK_BETA = 15.0 / 16.0
SWEEP_SPEED = 0.75
STRETCH_RATE = 0.375
HALO = 3
PAD = 8


def first_derivative(shifted):
    return (
        45.0 * (shifted(1) - shifted(-1))
        - 9.0 * (shifted(2) - shifted(-2))
        + (shifted(3) - shifted(-3))
    ) / 60.0


def second_derivative(shifted):
    return (
        -49.0 / 18.0 * shifted(0)
        + 1.5 * (shifted(1) + shifted(-1))
        - 0.15 * (shifted(2) + shifted(-2))
        + (shifted(3) + shifted(-3)) / 90.0
    )


def test_pattern(field_index, planes):
    height = jnp.arange(planes).astype(jnp.float32)
    wavenumber = (field_index // 4 + 1).astype(jnp.float32)
    phase = 2.0 * math.pi * wavenumber[:, None] * height[None, :] / planes
    profile = jnp.where((field_index // 2 % 2 == 0)[:, None], jnp.cos(phase), jnp.sin(phase))
    component = field_index % 2
    selector = (jnp.arange(3)[None, :] == component[:, None]).astype(jnp.float32)
    return (selector[:, :, None] * profile[:, None, :])[:, :, :, None, None]


def cross_emf(velocity, summed):
    vel = velocity.astype(jnp.float32)
    fld = summed.astype(jnp.float32)
    emf_x = vel[1] * fld[:, 2] - vel[2] * fld[:, 1]
    emf_y = vel[2] * fld[:, 0] - vel[0] * fld[:, 2]
    emf_z = vel[0] * fld[:, 1] - vel[1] * fld[:, 0]
    return jnp.stack([emf_x, emf_y, emf_z], 1).astype(jnp.bfloat16)


def _bf(x):
    return x.astype(jnp.bfloat16).astype(jnp.float32)


def make_kernel(planes, rows, width, fi, aliased):
    ext_w = width + 256

    def kernel(pat_ref, f_hbm, fb_ref, fa_ref, r_ref, v_hbm, g_ref, *rest):
        if aliased:
            rest = rest[2:]
        nf_ref, nr_ref, fs, es, v_ref, sems = rest

        def copy_f(zz):
            return pltpu.make_async_copy(
                f_hbm.at[fi, :, zz], fs.at[:, zz, pl.ds(PAD, rows), :], sems.at[0, zz]
            )

        def copy_v(zz):
            return pltpu.make_async_copy(v_hbm.at[:, zz], v_ref.at[:, zz], sems.at[1, zz])

        def fill_halo():
            for zz in range(planes):
                for c in range(3):
                    at = (c * planes + zz) * HALO
                    got_b = fb_ref[at : at + HALO, :].astype(jnp.float32)
                    got_a = fa_ref[at : at + HALO, :].astype(jnp.float32)
                    fs[c, zz, PAD - HALO : PAD, :] = got_b
                    fs[c, zz, PAD + rows : PAD + rows + HALO, :] = got_a

        def fill(z, carry):
            copy_f(z).wait()
            copy_v(z).wait()
            s = [_bf(fs[c, z] + pat_ref[fi, c * planes + z]) for c in range(3)]
            v = [v_ref[c, z].astype(jnp.float32) for c in range(3)]
            es[0, z] = _bf(v[1] * s[2] - v[2] * s[1])
            es[1, z] = _bf(v[2] * s[0] - v[0] * s[2])
            es[2, z] = _bf(v[0] * s[1] - v[1] * s[0])
            return carry

        z = pl.program_id(0)

        @pl.when(z == 0)
        def _():
            fill_halo()
            for zz in range(planes):
                copy_f(zz).start()
                copy_v(zz).start()
            lax.fori_loop(0, planes, fill, 0)

        xpos = lax.broadcasted_iota(jnp.int32, (8, width), 1).astype(jnp.float32)
        sweep = -SWEEP_SPEED * (2.0 * xpos / (width - 1) - 1.0)

        def step(z):
            zi = {o: lax.rem(z + o + planes, planes) for o in range(-HALO, HALO + 1)}
            for h in range(rows // 8):
                r0 = PAD + 8 * h

                def ysh(buf, c):
                    return lambda o: buf[c, z, pl.ds(r0 + o, 8), :]

                def zsh(buf, c):
                    return lambda o: buf[c, zi[o], pl.ds(r0, 8), :]

                def xsh(buf, c, gch):
                    g = g_ref[0, gch, z, pl.ds(8 * h, 8), :]
                    ext = jnp.concatenate([g, buf[c, z, pl.ds(r0, 8), :], g], axis=-1)

                    def shifted(o):
                        if o == 0:
                            return buf[c, z, pl.ds(r0, 8), :]
                        return pltpu.roll(ext, (-o) % ext_w, 1)[:, 128 : 128 + width]

                    return shifted

                curl = [
                    first_derivative(ysh(es, 2)) - first_derivative(zsh(es, 1)),
                    first_derivative(zsh(es, 0)) - first_derivative(xsh(es, 2, 5)),
                    first_derivative(xsh(es, 1, 4)) - first_derivative(ysh(es, 0)),
                ]
                centre0 = fs[0, z, pl.ds(r0, 8), :]
                for c in range(3):
                    laplace = (
                        second_derivative(xsh(fs, c, c))
                        + second_derivative(ysh(fs, c))
                        + second_derivative(zsh(fs, c))
                    )
                    field_dy = first_derivative(ysh(fs, c))
                    rate = curl[c] + DIFFUSIVITY * laplace - sweep * field_dy
                    if c == 1:
                        rate = rate + (-STRETCH_RATE) * centre0
                    reg = r_ref[0, c, 0, pl.ds(8 * h, 8), :]
                    new_reg = RK_ALPHA * reg + TIME_STEP * rate
                    centre = fs[c, z, pl.ds(r0, 8), :]
                    nr_ref[0, c, 0, pl.ds(8 * h, 8), :] = new_reg
                    nf_ref[0, c, 0, pl.ds(8 * h, 8), :] = centre + RK_BETA * new_reg

        step(z)

    return kernel


def stencil(fi, pat, field, fb8, fa8, register, vel32, ghost, prev):
    fields, _, planes, rows, width = field.shape
    blk = lambda r: pl.BlockSpec((1, 3, planes, r, width), lambda i: (fi, 0, 0, 0, 0))
    one = lambda r: pl.BlockSpec((1, 3, planes, r, width), lambda i: (0, 0, 0, 0, 0))
    per_z = pl.BlockSpec((1, 3, 1, rows, width), lambda i: (fi, 0, i, 0, 0))
    out_sds = jax.ShapeDtypeStruct(field.shape, jnp.float32)
    in_specs = [
        pl.BlockSpec(memory_space=pltpu.SMEM),
        pl.BlockSpec(memory_space=pl.ANY),
        pl.BlockSpec(memory_space=pltpu.VMEM),
        pl.BlockSpec(memory_space=pltpu.VMEM),
        per_z,
        pl.BlockSpec(memory_space=pl.ANY),
        pl.BlockSpec((1, 6, planes, rows, 128), lambda i: (fi, 0, 0, 0, 0)),
    ]
    args = [pat, field, fb8, fa8, register, vel32, ghost]
    aliases = {}
    if prev is not None:
        in_specs += [pl.BlockSpec(memory_space=pl.ANY)] * 2
        args += list(prev)
        aliases = {7: 0, 8: 1}
    return pl.pallas_call(
        make_kernel(planes, rows, width, fi, prev is not None),
        grid=(planes,),
        in_specs=in_specs,
        out_specs=[per_z, per_z],
        out_shape=[out_sds, out_sds],
        scratch_shapes=[
            pltpu.VMEM((3, planes, rows + 2 * PAD, width), jnp.float32),
            pltpu.VMEM((3, planes, rows + 2 * PAD, width), jnp.float32),
            pltpu.VMEM(vel32.shape, vel32.dtype),
            pltpu.SemaphoreType.DMA((2, planes)),
        ],
        input_output_aliases=aliases,
        cost_estimate=pl.CostEstimate(
            flops=200 * field.size // fields,
            transcendentals=0,
            bytes_accessed=16 * field.size // fields,
        ),
        compiler_params=pltpu.CompilerParams(
            dimension_semantics=("arbitrary",), vmem_limit_bytes=64000 * 1024
        ),
    )(*args)


def body(test_field, register, velocity, shear_shift):
    fields, _, planes, rows, width = test_field.shape
    tiles = lax.axis_size("tile")
    tile = lax.axis_index("tile")
    total_rows = tiles * rows
    up = [(i, (i + 1) % tiles) for i in range(tiles)]
    down = [((i + 1) % tiles, i) for i in range(tiles)]

    field_index = lax.axis_index("tf") * fields + jnp.arange(fields)
    pattern = test_pattern(field_index, planes)
    pat = pattern.reshape(fields, 3 * planes)

    halo_dt = jnp.bfloat16
    n_f = fields * 3 * planes * HALO
    n_v = 3 * velocity.shape[1] * HALO

    edges = lax.optimization_barrier(
        (test_field[..., rows - HALO :, :], test_field[..., :HALO, :])
    )

    def halo_rows(f, sl):
        edge = edges[0] if sl.start else edges[1]
        f_part = edge[f].astype(halo_dt).reshape(3 * planes * HALO, width)
        if f > 0:
            return f_part
        v_part = velocity[:, :, sl, :].reshape(n_v, width)
        return jnp.concatenate([f_part, v_part], axis=0)

    n_1 = 3 * planes * HALO
    got = []
    for f in range(fields):
        got_b = lax.ppermute(halo_rows(f, slice(rows - HALO, rows)), "tile", up)
        got_a = lax.ppermute(halo_rows(f, slice(0, HALO)), "tile", down)
        if f == 0:
            vb = got_b[n_1:].reshape(3, velocity.shape[1], HALO, width)
            va = got_a[n_1:].reshape(3, velocity.shape[1], HALO, width)
        got.append((got_b[:n_1], got_a[:n_1]))

    def padded(pair):
        return pair

    vext = jnp.pad(
        jnp.concatenate([vb, velocity, va], axis=2),
        ((0, 0), (0, 0), (PAD - HALO, PAD - HALO), (0, 0)),
    )
    vel32 = lax.all_gather(vext, "tf", axis=1, tiled=True)

    strip_f = jnp.concatenate([test_field[..., width - HALO :], test_field[..., :HALO]], axis=-1)
    strip_v = jnp.concatenate([velocity[..., width - HALO :], velocity[..., :HALO]], axis=-1)
    strip_v = lax.all_gather(strip_v, "tf", axis=1, tiled=True)
    strip_e = cross_emf(strip_v, (strip_f + pattern).astype(jnp.bfloat16)).astype(jnp.float32)
    comb = jnp.concatenate([strip_f, strip_e], axis=1)
    chans = HALO * fields * 6
    packed = jnp.transpose(comb, (4, 0, 1, 2, 3)).reshape(1, 2 * chans, planes * rows)
    gathered = lax.all_gather(packed, "tile", axis=0, tiled=True)
    row_of = lax.broadcasted_iota(jnp.int32, (chans, planes * rows), 1) % rows

    def select(part, shift):
        start = (tile * rows + shift) % total_rows
        first = start // rows
        offset = start % rows
        near = lax.dynamic_index_in_dim(part, first, 0, keepdims=False)
        far = lax.dynamic_index_in_dim(part, (first + 1) % tiles, 0, keepdims=False)
        near = jnp.roll(near, -offset, axis=1)
        far = jnp.roll(far, rows - offset, axis=1)
        picked = jnp.where(row_of + offset < rows, near, far)
        return picked.reshape(HALO, fields, 6, planes, rows)

    lo = select(gathered[:, :chans], shear_shift[0])
    hi = select(gathered[:, chans:], shear_shift[1])
    lane = lax.broadcasted_iota(jnp.int32, (1, 1, 1, 1, 128), 4)
    ghost = jnp.zeros((fields, 6, planes, rows, 128), jnp.float32)
    for j in range(HALO):
        ghost = jnp.where(lane == j, hi[j][..., None], ghost)
        ghost = jnp.where(lane == 128 - HALO + j, lo[j][..., None], ghost)

    prev = None
    for f in range(fields):
        pair = got[f]
        if prev is not None:
            pair, prev = lax.optimization_barrier((pair, prev))
        fb, fa = padded(pair)
        prev = stencil(f, pat, test_field, fb, fa, register, vel32, ghost, prev)
    new_field, new_register = prev
    return (new_field, new_register)


def solution(mesh):
    return jax.shard_map(
        body,
        mesh=mesh,
        in_specs=(
            P("tf", None, None, "tile", None),
            P("tf", None, None, "tile", None),
            P(None, "tf", "tile", None),
            P(),
        ),
        out_specs=(P("tf", None, None, "tile", None), P("tf", None, None, "tile", None)),
        check_vma=False,
    )
```
